256 devices in a mesh: pipe: 8 (over z), seq: 32 (over y, x, core).
Axes of the slice: x: 4, y: 4, z: 8, core: 2. Of those that a mesh axis runs over, the one named last changes fastest.
Arguments:
- queries: bfloat16 [8, 4096, 8192], P('pipe', 'seq'), may hold values from -47.6 to 47.6
- keys: bfloat16 [8, 4096, 1024], P('pipe', 'seq'), may hold values from -4 to 4
- values: bfloat16 [8, 4096, 1024], P('pipe', 'seq'), may hold values from -6 to 6
- out_grad: bfloat16 [8, 4096, 8192], P('pipe', 'seq'), may hold values from -6 to 6
- window_blocks: int32 [64, 3], replicated, may hold values from 0 to 63, as said below
- global_blocks: int32 [64, 2], replicated, may hold values from 0 to 63, as said below
- random_blocks: int32 [64, 3], replicated, may hold values from 0 to 63
Outputs:
- handed_queries: bfloat16 [8, 4096, 8192], P('pipe', 'seq')
- handed_keys: bfloat16 [8, 4096, 1024], P('pipe', 'seq')
- handed_values: bfloat16 [8, 4096, 1024], P('pipe', 'seq')
The draws below stay inside these ranges and needn't reach their ends.
Inputs may be any that keep to these rules, and one draw needn't show every extreme that they name: `window_blocks`: row b lists b - 1, b, b + 1; a neighbour that lies in another document of the pack, or outside the sequence, is replaced by b. `global_blocks`: every row lists the same two blocks: one below 64 // 2, and the last block 64 - 1.
All inputs are finite; a program needn't handle non-finite values.
Results may differ from the reference program's by a relative error of at most 0.012.
The reference program's roundings to bfloat16 on the way count: a program that leaves them out, or rounds other values in their place, can miss the bound.
Values may be sent and summed in bfloat16 or wider, within the bound.
No kernel may reach another device: no remote copies, remote signals or barrier semaphores. Data moves between devices by JAX's collectives and lax.ppermute only.
A program may use at most 128 MiB of HBM per device.

```python
import jax
import jax.numpy as jnp
from jax import lax

HEADS = 64
KV = 8
HD = 128
BLOCK = 64
RAND = 3
SEQLEN = 4096
NB = 64
N_PIPE = 8


def paired_draw(key):
    first = jax.random.fold_in(key, 11)
    second = jax.random.fold_in(key, 12)
    key_rows = jnp.clip(jax.random.normal(first, (N_PIPE, SEQLEN, KV, HD), jnp.float32), -4.0, 4.0)
    query_rows = jnp.clip(jax.random.normal(second, (N_PIPE, SEQLEN, HEADS, HD), jnp.float32), -4.0, 4.0)
    return (query_rows.reshape(N_PIPE, SEQLEN, HEADS * HD), key_rows.reshape(N_PIPE, SEQLEN, KV * HD))


def draw_queries(key, part):
    return paired_draw(key)[0].astype(jnp.bfloat16)


def draw_keys(key, part):
    return paired_draw(key)[1].astype(jnp.bfloat16)


def draw_window_blocks(key, part):
    begins = jax.random.randint(jax.random.fold_in(key, 31), (NB,), 0, 4) == 0
    segment = jnp.cumsum(begins.astype(jnp.int32))
    index = jnp.arange(NB, dtype=jnp.int32)
    seg_prev = jnp.concatenate([segment[:1] - 1, segment[:-1]])
    seg_next = jnp.concatenate([segment[1:], segment[-1:] + 1])
    left = jnp.where(seg_prev == segment, index - 1, index)
    right = jnp.where(seg_next == segment, index + 1, index)
    return jnp.stack([left, index, right], axis=1).astype(jnp.int32)


def draw_global_blocks(key, part):
    lower = jax.random.randint(jax.random.fold_in(key, 41), (), 0, NB // 2)
    upper = jnp.zeros((), jnp.int32) + (NB - 1)
    pair = jnp.stack([lower.astype(jnp.int32), upper]).astype(jnp.int32)
    return jnp.zeros((NB, 2), jnp.int32) + pair[None, :]


def place_ends(drawn, key, smallest, largest):
    extent = drawn.shape
    spot = [jax.random.randint(jax.random.fold_in(key, axis), (), 0, extent[axis]) for axis in range(len(extent))]
    drawn = drawn.at[tuple(spot)].set(smallest)
    longest = extent.index(max(extent))
    spot[longest] = (spot[longest] + 1) % extent[longest]
    return drawn.at[tuple(spot)].set(largest)


def level_of(key, shape, pieces, smallest, largest):
    loudness = 1.0
    for dim, parts in pieces:
        steps = jax.random.uniform(jax.random.fold_in(jax.random.fold_in(key, 6), dim), (parts,), jnp.float32, smallest / len(pieces), largest / len(pieces))
        loudness = loudness * jnp.repeat(jnp.exp(steps), shape[dim] // parts).reshape((-1,) + (1,) * (len(shape) - 1 - dim))
    return loudness


def centred(stream_key, dims, deviation, reach, pieces=(), kind=jnp.bfloat16):
    drawn = deviation * jax.random.normal(stream_key, dims, jnp.float32)
    if pieces:
        drawn = drawn * level_of(stream_key, dims, pieces, -0.22, 0.18)
    return jnp.clip(drawn, -reach, reach).astype(kind)


def setup_inputs(seed: int = 0) -> dict:
    key_list = jax.random.split(jax.random.key(seed), 8)
    queries = draw_queries(jax.random.fold_in(key_list[7], 71), 0)
    keys = draw_keys(jax.random.fold_in(key_list[7], 71), 0)
    values = centred(key_list[2], (N_PIPE, SEQLEN, KV * HD), 1.0, 6.0, ((0, 8), (1, 32)))
    out_grad = centred(key_list[3], (N_PIPE, SEQLEN, HEADS * HD), 1.0, 6.0, ((0, 8), (1, 32)))
    window_blocks = draw_window_blocks(jax.random.fold_in(key_list[7], 71), 0)
    global_blocks = draw_global_blocks(jax.random.fold_in(key_list[7], 71), 0)
    random_blocks = place_ends(jax.random.randint(key_list[6], (NB, RAND), 0, NB), jax.random.fold_in(key_list[6], 1), 0, NB - 1).astype(jnp.int32)
    return dict(queries=queries, keys=keys, values=values, out_grad=out_grad, window_blocks=window_blocks, global_blocks=global_blocks, random_blocks=random_blocks)


def block_lists(window_blocks, global_blocks, random_blocks):
    listed = jnp.concatenate([window_blocks, global_blocks, random_blocks], axis=1).astype(jnp.int32)
    width = listed.shape[1]
    same = listed[:, :, None] == listed[:, None, :]
    earlier = jnp.arange(width)[None, :] < jnp.arange(width)[:, None]
    repeated = jnp.any(jnp.logical_and(same, earlier[None]), axis=2)
    return listed, jnp.logical_not(repeated)


def block_grads(q_rows, g_rows, k_blocks, v_blocks, listed, live):
    count = listed.shape[0]
    slots = listed.shape[1]
    scale = HD ** -0.5
    k_near = k_blocks[listed].reshape(count, slots * BLOCK, HD).astype(jnp.float32)
    v_near = v_blocks[listed].reshape(count, slots * BLOCK, HD).astype(jnp.float32)
    q_wide = q_rows.astype(jnp.float32)
    g_wide = g_rows.astype(jnp.float32)
    allowed = jnp.repeat(live, BLOCK, axis=1)[:, None, :]
    scores = jnp.einsum("grd,gsd->grs", q_wide, k_near) * scale
    scores = jnp.where(allowed, scores, -jnp.inf)
    top = jnp.max(scores, axis=-1, keepdims=True)
    expd = jnp.exp(scores - top)
    probs = expd / jnp.sum(expd, axis=-1, keepdims=True)
    probs_low = lax.optimization_barrier(probs.astype(jnp.bfloat16)).astype(jnp.float32)
    attn_out = jnp.einsum("grs,gsd->grd", probs_low, v_near).astype(jnp.bfloat16)
    attn_out = lax.optimization_barrier(attn_out).astype(jnp.float32)
    delta = jnp.sum(g_wide * attn_out, axis=-1, keepdims=True)
    dprobs = jnp.einsum("grd,gsd->grs", g_wide, v_near)
    ds_low = lax.optimization_barrier((probs * (dprobs - delta)).astype(jnp.bfloat16)).astype(jnp.float32)
    grad_q = (jnp.einsum("grs,gsd->grd", ds_low, k_near) * scale).astype(jnp.bfloat16)
    dk_slots = jnp.einsum("grs,grd->gsd", ds_low, q_wide) * scale
    dv_slots = jnp.einsum("grs,grd->gsd", probs_low, g_wide)
    nblocks = k_blocks.shape[0]
    grad_k = jnp.zeros((nblocks, BLOCK, HD), jnp.float32).at[listed].add(dk_slots.reshape(count, slots, BLOCK, HD))
    grad_v = jnp.zeros((nblocks, BLOCK, HD), jnp.float32).at[listed].add(dv_slots.reshape(count, slots, BLOCK, HD))
    return grad_q, grad_k, grad_v


def reference(queries, keys, values, out_grad, window_blocks, global_blocks, random_blocks):
    listed, live = block_lists(window_blocks, global_blocks, random_blocks)
    seqlen = queries.shape[1]
    nblocks = seqlen // BLOCK
    group = HEADS // KV

    def one_group(items):
        q_head, g_head, k_head, v_head = items
        q_rows = q_head.reshape(nblocks, BLOCK * group, HD)
        g_rows = g_head.reshape(nblocks, BLOCK * group, HD)
        k_blocks = k_head.reshape(nblocks, BLOCK, HD)
        v_blocks = v_head.reshape(nblocks, BLOCK, HD)
        grad_q, grad_k, grad_v = block_grads(q_rows, g_rows, k_blocks, v_blocks, listed, live)
        return (grad_q.reshape(seqlen, group, HD), grad_k.astype(jnp.bfloat16).reshape(seqlen, HD),
                grad_v.astype(jnp.bfloat16).reshape(seqlen, HD))

    def one_section(items):
        q_section, g_section, k_section, v_section = items
        q_split = q_section.reshape(seqlen, KV, group, HD).transpose(1, 0, 2, 3)
        g_split = g_section.reshape(seqlen, KV, group, HD).transpose(1, 0, 2, 3)
        k_split = k_section.reshape(seqlen, KV, HD).transpose(1, 0, 2)
        v_split = v_section.reshape(seqlen, KV, HD).transpose(1, 0, 2)
        grad_q, grad_k, grad_v = lax.map(one_group, (q_split, g_split, k_split, v_split))
        return (grad_q.transpose(1, 0, 2, 3).reshape(seqlen, HEADS * HD),
                grad_k.transpose(1, 0, 2).reshape(seqlen, KV * HD),
                grad_v.transpose(1, 0, 2).reshape(seqlen, KV * HD))

    grad_q, grad_k, grad_v = lax.map(one_section, (queries, out_grad, keys, values))
    handed_queries = jnp.concatenate([grad_q[1:], jnp.zeros_like(grad_q[:1])], axis=0)
    handed_keys = jnp.concatenate([grad_k[1:], jnp.zeros_like(grad_k[:1])], axis=0)
    handed_values = jnp.concatenate([grad_v[1:], jnp.zeros_like(grad_v[:1])], axis=0)
    return (handed_queries, handed_keys, handed_values)
```

```python
import functools

import jax
import jax.numpy as jnp
from jax import lax
from jax.experimental import pallas as pl
from jax.experimental.pallas import tpu as pltpu
from jax.sharding import PartitionSpec as P

HEADS = 64
KV = 8
HD = 128
BLOCK = 64
INTERPRET = False


def from_behind(block, axis, distance):
    devices = range(lax.axis_size(axis))
    route = [(i - distance, i) for i in devices if i - distance in devices]
    return lax.ppermute(block, axis, route)


def block_lists(window_blocks, global_blocks, random_blocks):
    listed = jnp.concatenate([window_blocks, global_blocks, random_blocks], axis=1)
    width = listed.shape[1]
    same = listed[:, :, None] == listed[:, None, :]
    earlier = jnp.arange(width)[None, :] < jnp.arange(width)[:, None]
    repeated = jnp.any(jnp.logical_and(same, earlier[None]), axis=2)
    return (listed, jnp.logical_not(repeated))


def grads_kernel(slots, rows, listed_ref, live_ref, q_ref, g_ref, k_ref, v_ref,
                 dq_ref, dkv_ref, kc_ref, vc_ref):
    b = pl.program_id(0)
    scale = HD ** (-0.5)
    width = slots * BLOCK

    @pl.when(b == 0)
    def _():
        dkv_ref[...] = jnp.zeros(dkv_ref.shape, dkv_ref.dtype)

    starts = []
    lives = []
    for j in range(slots):
        start = pl.multiple_of(listed_ref[b * slots + j] * BLOCK, BLOCK)
        starts.append(start)
        lives.append(live_ref[b * slots + j])
        kc_ref[j * BLOCK:(j + 1) * BLOCK, :] = k_ref[pl.ds(start, BLOCK), :]
        vc_ref[j * BLOCK:(j + 1) * BLOCK, :] = v_ref[pl.ds(start, BLOCK), :]

    q = q_ref[...]
    g = g_ref[...]
    kc = kc_ref[...]
    vc = vc_ref[...]
    col = lax.broadcasted_iota(jnp.int32, (1, width), 1)
    live_cols = jnp.zeros((1, width), jnp.int32)
    for j in range(slots):
        inside = jnp.logical_and(col >= j * BLOCK, col < (j + 1) * BLOCK)
        live_cols = jnp.where(inside, lives[j], live_cols)
    nt = (((1,), (1,)), ((), ()))
    tn = (((0,), (0,)), ((), ()))
    scores = lax.dot_general(q, kc, nt, preferred_element_type=jnp.float32) * scale
    scores = jnp.where(live_cols != 0, scores, -jnp.inf)
    top = jnp.max(scores, axis=-1, keepdims=True)
    expd = jnp.exp(scores - top)
    probs = expd / jnp.sum(expd, axis=-1, keepdims=True)
    probs_low = probs.astype(jnp.bfloat16)
    attn = jnp.dot(probs_low, vc, preferred_element_type=jnp.float32)
    attn = attn.astype(jnp.bfloat16).astype(jnp.float32)
    delta = jnp.sum(g.astype(jnp.float32) * attn, axis=-1, keepdims=True)
    dprobs = lax.dot_general(g, vc, nt, preferred_element_type=jnp.float32)
    ds_low = (probs * (dprobs - delta)).astype(jnp.bfloat16)
    dq = jnp.dot(ds_low, kc, preferred_element_type=jnp.float32) * scale
    dq_ref[...] = dq.astype(jnp.bfloat16)
    dk_slots = lax.dot_general(ds_low, q, tn, preferred_element_type=jnp.float32) * scale
    dv_slots = lax.dot_general(probs_low, g, tn, preferred_element_type=jnp.float32)
    for j in range(slots):
        @pl.when(lives[j] != 0)
        def _():
            window = pl.ds(starts[j], BLOCK)
            dkv_ref[0, window, :] += dk_slots[j * BLOCK:(j + 1) * BLOCK, :]
            dkv_ref[1, window, :] += dv_slots[j * BLOCK:(j + 1) * BLOCK, :]


def block_grads(q_rows, g_rows, k_head, v_head, listed, live):
    nblocks, slots = listed.shape
    seqlen = k_head.shape[0]
    rows = q_rows.shape[0] // nblocks
    kernel = functools.partial(grads_kernel, slots, rows)
    grid_spec = pltpu.PrefetchScalarGridSpec(
        num_scalar_prefetch=2,
        grid=(nblocks,),
        in_specs=[
            pl.BlockSpec((rows, HD), lambda b, *_: (b, 0)),
            pl.BlockSpec((rows, HD), lambda b, *_: (b, 0)),
            pl.BlockSpec((seqlen, HD), lambda b, *_: (0, 0)),
            pl.BlockSpec((seqlen, HD), lambda b, *_: (0, 0)),
        ],
        out_specs=[
            pl.BlockSpec((rows, HD), lambda b, *_: (b, 0)),
            pl.BlockSpec((2, seqlen, HD), lambda b, *_: (0, 0, 0)),
        ],
        scratch_shapes=[
            pltpu.VMEM((slots * BLOCK, HD), jnp.bfloat16),
            pltpu.VMEM((slots * BLOCK, HD), jnp.bfloat16),
        ],
    )
    return pl.pallas_call(
        kernel,
        grid_spec=grid_spec,
        out_shape=[
            jax.ShapeDtypeStruct(q_rows.shape, jnp.bfloat16),
            jax.ShapeDtypeStruct((2, seqlen, HD), jnp.float32),
        ],
        compiler_params=pltpu.CompilerParams(dimension_semantics=("arbitrary",)),
        interpret=INTERPRET,
    )(listed.reshape(-1), live.reshape(-1).astype(jnp.int32), q_rows, g_rows, k_head, v_head)


def body(queries, keys, values, out_grad, window_blocks, global_blocks, random_blocks):
    lanes = lax.axis_size("seq")
    tok = queries.shape[1]
    repeat = lanes // KV
    q_local = queries[0].reshape(tok, HEADS, HD)
    g_local = out_grad[0].reshape(tok, HEADS, HD)
    q_heads, g_heads = (
        lax.all_to_all(q_local, "seq", split_axis=1, concat_axis=0, tiled=True),
        lax.all_to_all(g_local, "seq", split_axis=1, concat_axis=0, tiled=True),
    )
    k_rep = jnp.repeat(keys[0].reshape(tok, KV, HD), repeat, axis=1)
    v_rep = jnp.repeat(values[0].reshape(tok, KV, HD), repeat, axis=1)
    kv_send = jnp.stack([k_rep, v_rep], axis=2)
    kv_head = lax.all_to_all(kv_send, "seq", split_axis=1, concat_axis=0, tiled=True)
    k_head = kv_head[:, 0, 0, :]
    v_head = kv_head[:, 0, 1, :]
    seqlen = q_heads.shape[0]
    per_device = q_heads.shape[1]
    listed, live = block_lists(window_blocks, global_blocks, random_blocks)
    q_rows = q_heads.reshape(seqlen * per_device, HD)
    g_rows = g_heads.reshape(seqlen * per_device, HD)
    dq_rows, dkv = block_grads(q_rows, g_rows, k_head, v_head, listed, live)
    dq_heads = dq_rows.reshape(seqlen, per_device, HD)
    dq_tokens = lax.all_to_all(dq_heads, "seq", split_axis=0, concat_axis=1, tiled=True)
    dkv_parts = lax.all_to_all(dkv, "seq", split_axis=1, concat_axis=0, tiled=True)
    dkv_sum = jnp.sum(dkv_parts.reshape(KV, repeat, 2, tok, HD), axis=1).astype(jnp.bfloat16)
    dk_tokens = dkv_sum[:, 0].transpose(1, 0, 2)
    dv_tokens = dkv_sum[:, 1].transpose(1, 0, 2)
    dq_flat = dq_tokens.reshape(1, tok, HEADS * HD)
    dk_flat = dk_tokens.reshape(1, tok, KV * HD)
    dv_flat = dv_tokens.reshape(1, tok, KV * HD)
    return from_behind((dq_flat, dk_flat, dv_flat), "pipe", -1)


def solution(mesh):
    in_specs = (
        P("pipe", "seq", None),
        P("pipe", "seq", None),
        P("pipe", "seq", None),
        P("pipe", "seq", None),
        P(),
        P(),
        P(),
    )
    out_specs = (P("pipe", "seq", None), P("pipe", "seq", None), P("pipe", "seq", None))
    return jax.shard_map(body, mesh=mesh, in_specs=in_specs, out_specs=out_specs, check_vma=False)
```

```python
import functools

import jax
import jax.numpy as jnp
from jax import lax
from jax.experimental import pallas as pl
from jax.experimental.pallas import tpu as pltpu
from jax.sharding import PartitionSpec as P

HEADS = 64
KV = 8
HD = 128
BLOCK = 64
INTERPRET = False


def from_behind(block, axis, distance):
    devices = range(lax.axis_size(axis))
    route = [(i - distance, i) for i in devices if i - distance in devices]
    return lax.ppermute(block, axis, route)


def block_lists(window_blocks, global_blocks, random_blocks):
    listed = jnp.concatenate([window_blocks, global_blocks, random_blocks], axis=1)
    width = listed.shape[1]
    same = listed[:, :, None] == listed[:, None, :]
    earlier = jnp.arange(width)[None, :] < jnp.arange(width)[:, None]
    repeated = jnp.any(jnp.logical_and(same, earlier[None]), axis=2)
    return (listed, jnp.logical_not(repeated))


def grads_kernel(slots, chained, listed_ref, live_ref, q_ref, g_ref, k_ref, v_ref, *refs):
    if chained:
        dkv_in_ref, dq_ref, dkv_ref, kc_ref, vc_ref = refs
    else:
        dq_ref, dkv_ref, kc_ref, vc_ref = refs
    b = pl.program_id(0)
    scale = HD ** (-0.5)
    width = slots * BLOCK

    @pl.when(b == 0)
    def _():
        if chained:
            dkv_ref[...] = dkv_in_ref[...]
        else:
            dkv_ref[...] = jnp.zeros(dkv_ref.shape, dkv_ref.dtype)

    starts = []
    lives = []
    for j in range(slots):
        start = pl.multiple_of(listed_ref[b * slots + j] * BLOCK, BLOCK)
        starts.append(start)
        lives.append(live_ref[b * slots + j])
        kc_ref[j * BLOCK:(j + 1) * BLOCK, :] = k_ref[pl.ds(start, BLOCK), :]
        vc_ref[j * BLOCK:(j + 1) * BLOCK, :] = v_ref[pl.ds(start, BLOCK), :]

    q = q_ref[...]
    g = g_ref[...]
    kc = kc_ref[...]
    vc = vc_ref[...]
    col = lax.broadcasted_iota(jnp.int32, (1, width), 1)
    live_cols = jnp.zeros((1, width), jnp.int32)
    for j in range(slots):
        inside = jnp.logical_and(col >= j * BLOCK, col < (j + 1) * BLOCK)
        live_cols = jnp.where(inside, lives[j], live_cols)
    nt = (((1,), (1,)), ((), ()))
    tn = (((0,), (0,)), ((), ()))
    scores = lax.dot_general(q, kc, nt, preferred_element_type=jnp.float32) * scale
    scores = jnp.where(live_cols != 0, scores, -jnp.inf)
    top = jnp.max(scores, axis=-1, keepdims=True)
    expd = jnp.exp(scores - top)
    probs = expd / jnp.sum(expd, axis=-1, keepdims=True)
    probs_low = probs.astype(jnp.bfloat16)
    attn = jnp.dot(probs_low, vc, preferred_element_type=jnp.float32)
    attn = attn.astype(jnp.bfloat16).astype(jnp.float32)
    delta = jnp.sum(g.astype(jnp.float32) * attn, axis=-1, keepdims=True)
    dprobs = lax.dot_general(g, vc, nt, preferred_element_type=jnp.float32)
    ds_low = (probs * (dprobs - delta)).astype(jnp.bfloat16)
    dq = jnp.dot(ds_low, kc, preferred_element_type=jnp.float32) * scale
    dq_ref[...] = dq.astype(jnp.bfloat16)
    dk_slots = lax.dot_general(ds_low, q, tn, preferred_element_type=jnp.float32) * scale
    dv_slots = lax.dot_general(probs_low, g, tn, preferred_element_type=jnp.float32)
    for j in range(slots):
        @pl.when(lives[j] != 0)
        def _():
            window = pl.ds(starts[j], BLOCK)
            dkv_ref[0, window, :] += dk_slots[j * BLOCK:(j + 1) * BLOCK, :]
            dkv_ref[1, window, :] += dv_slots[j * BLOCK:(j + 1) * BLOCK, :]


def block_grads(qg_rows, kv_head, listed, live, dkv_in=None):
    nblocks, slots = listed.shape
    seqlen = kv_head.shape[1]
    rows = qg_rows.shape[1] // nblocks
    chained = dkv_in is not None
    width = slots * BLOCK
    kernel = functools.partial(grads_kernel, slots, chained)
    in_specs = [
        pl.BlockSpec((None, rows, HD), lambda b, *_: (0, b, 0)),
        pl.BlockSpec((None, rows, HD), lambda b, *_: (1, b, 0)),
        pl.BlockSpec((None, seqlen, HD), lambda b, *_: (0, 0, 0)),
        pl.BlockSpec((None, seqlen, HD), lambda b, *_: (1, 0, 0)),
    ]
    operands = [qg_rows, qg_rows, kv_head, kv_head]
    if chained:
        in_specs.append(pl.BlockSpec((2, seqlen, HD), lambda b, *_: (0, 0, 0)))
        operands.append(dkv_in)
    grid_spec = pltpu.PrefetchScalarGridSpec(
        num_scalar_prefetch=2,
        grid=(nblocks,),
        in_specs=in_specs,
        out_specs=[
            pl.BlockSpec((rows, HD), lambda b, *_: (b, 0)),
            pl.BlockSpec((2, seqlen, HD), lambda b, *_: (0, 0, 0)),
        ],
        scratch_shapes=[
            pltpu.VMEM((slots * BLOCK, HD), jnp.bfloat16),
            pltpu.VMEM((slots * BLOCK, HD), jnp.bfloat16),
        ],
    )
    return pl.pallas_call(
        kernel,
        grid_spec=grid_spec,
        out_shape=[
            jax.ShapeDtypeStruct(qg_rows.shape[1:], jnp.bfloat16),
            jax.ShapeDtypeStruct((2, seqlen, HD), jnp.float32),
        ],
        compiler_params=pltpu.CompilerParams(dimension_semantics=("arbitrary",)),
        cost_estimate=pl.CostEstimate(
            flops=12 * nblocks * rows * width * HD,
            transcendentals=nblocks * rows * width,
            bytes_accessed=4 * qg_rows.size + 4 * kv_head.size + 16 * seqlen * HD,
        ),
        interpret=INTERPRET,
    )(listed.reshape(-1), live.reshape(-1).astype(jnp.int32), *operands)


SEQ = ("y", "xh", "xl", "core")
NEAR = ("xl", "core")
FAR = ("y", "xh")


def body(queries, keys, values, out_grad, window_blocks, global_blocks, random_blocks):
    lanes = lax.axis_size(SEQ)
    near = lax.axis_size(NEAR)
    far = lax.axis_size(FAR)
    tok = queries.shape[1]
    seqlen = tok * lanes
    per_device = HEADS // lanes
    kv_local = jnp.stack([keys[0].reshape(tok, KV, HD), values[0].reshape(tok, KV, HD)])
    kv_send = kv_local.transpose(2, 0, 1, 3)
    kv_far = lax.all_to_all(kv_send, FAR, split_axis=0, concat_axis=0, tiled=True)
    kv_all = lax.all_gather(kv_far, NEAR, axis=0, tiled=False)
    kv_head = kv_all.transpose(2, 1, 0, 3, 4).reshape(2, seqlen, HD)
    listed, live = block_lists(window_blocks, global_blocks, random_blocks)
    qg_local = jnp.stack([queries[0].reshape(tok, HEADS, HD), out_grad[0].reshape(tok, HEADS, HD)])
    qg_heads = lax.all_to_all(qg_local, SEQ, split_axis=2, concat_axis=1, tiled=True)
    qg_rows = qg_heads.reshape(2, seqlen * per_device, HD)
    dq_rows, dkv = block_grads(qg_rows, kv_head, listed, live)
    dq_heads = dq_rows.reshape(seqlen, per_device, HD)
    dq_tokens = lax.all_to_all(dq_heads, SEQ, split_axis=0, concat_axis=1, tiled=True)
    dkv_grouped = dkv.reshape(2, far, near, tok, HD).transpose(2, 0, 1, 3, 4)
    dkv_part = lax.psum_scatter(dkv_grouped, NEAR, scatter_dimension=0, tiled=True)
    dkv_low = dkv_part.reshape(2, far, tok, HD).astype(jnp.bfloat16)
    dkv_tokens = lax.all_to_all(dkv_low, FAR, split_axis=1, concat_axis=1, tiled=True)
    dk_tokens = dkv_tokens[0].transpose(1, 0, 2)
    dv_tokens = dkv_tokens[1].transpose(1, 0, 2)
    dq_flat = dq_tokens.reshape(1, tok, HEADS * HD)
    dk_flat = dk_tokens.reshape(1, tok, KV * HD)
    dv_flat = dv_tokens.reshape(1, tok, KV * HD)
    return from_behind((dq_flat, dk_flat, dv_flat), "pipe", -1)


def solution(mesh):
    pipe, lanes = mesh.devices.shape
    fine = mesh.devices.reshape(pipe, lanes // 8, 2, 2, 2)
    sub = jax.sharding.Mesh(fine, ("pipe",) + SEQ)
    block = P("pipe", SEQ, None)
    in_specs = (block, block, block, block, P(), P(), P())
    out_specs = (block, block, block)
    return jax.shard_map(body, mesh=sub, in_specs=in_specs, out_specs=out_specs, check_vma=False)
```

```python
import functools

import jax
import jax.numpy as jnp
from jax import lax
from jax.experimental import pallas as pl
from jax.experimental.pallas import tpu as pltpu
from jax.sharding import PartitionSpec as P

HEADS = 64
KV = 8
HD = 128
BLOCK = 64
INTERPRET = False


def from_behind(block, axis, distance):
    devices = range(lax.axis_size(axis))
    route = [(i - distance, i) for i in devices if i - distance in devices]
    return lax.ppermute(block, axis, route)


def block_lists(window_blocks, global_blocks, random_blocks):
    listed = jnp.concatenate([window_blocks, global_blocks, random_blocks], axis=1)
    width = listed.shape[1]
    same = listed[:, :, None] == listed[:, None, :]
    earlier = jnp.arange(width)[None, :] < jnp.arange(width)[:, None]
    repeated = jnp.any(jnp.logical_and(same, earlier[None]), axis=2)
    return (listed, jnp.logical_not(repeated))


def grads_kernel(slots, steps, listed_ref, live_ref, q_ref, g_ref, kv_ref, dq_ref, dkv_ref, kc_ref, vc_ref):
    b = pl.program_id(0)
    scale = HD ** (-0.5)
    width = slots * BLOCK
    rows = q_ref.shape[0] // steps
    half = kv_ref.shape[2] // BLOCK

    @pl.when(b == 0)
    def _():
        dkv_ref[...] = jnp.zeros(dkv_ref.shape, dkv_ref.dtype)

    col = lax.broadcasted_iota(jnp.int32, (1, width), 1)
    nt = (((1,), (1,)), ((), ()))
    tn = (((0,), (0,)), ((), ()))
    for i in range(steps):
        base = (b * steps + i) * slots
        owners = []
        offsets = []
        lives = []
        for j in range(slots):
            n = listed_ref[base + j]
            owners.append(n // half)
            offsets.append(pl.multiple_of((n % half) * BLOCK, BLOCK))
            lives.append(live_ref[base + j])
            kc_ref[j * BLOCK:(j + 1) * BLOCK, :] = kv_ref[owners[j], 0, pl.ds(offsets[j], BLOCK), :]
            vc_ref[j * BLOCK:(j + 1) * BLOCK, :] = kv_ref[owners[j], 1, pl.ds(offsets[j], BLOCK), :]
        q = q_ref[i * rows:(i + 1) * rows, :]
        g = g_ref[i * rows:(i + 1) * rows, :]
        kc = kc_ref[...]
        vc = vc_ref[...]
        live_cols = jnp.zeros((1, width), jnp.int32)
        for j in range(slots):
            inside = jnp.logical_and(col >= j * BLOCK, col < (j + 1) * BLOCK)
            live_cols = jnp.where(inside, lives[j], live_cols)
        scores = lax.dot_general(q, kc, nt, preferred_element_type=jnp.float32) * scale
        scores = jnp.where(live_cols != 0, scores, -jnp.inf)
        top = jnp.max(scores, axis=-1, keepdims=True)
        expd = jnp.exp(scores - top)
        probs = expd / jnp.sum(expd, axis=-1, keepdims=True)
        probs_low = probs.astype(jnp.bfloat16)
        attn = jnp.dot(probs_low, vc, preferred_element_type=jnp.float32)
        attn = attn.astype(jnp.bfloat16).astype(jnp.float32)
        delta = jnp.sum(g.astype(jnp.float32) * attn, axis=-1, keepdims=True)
        dprobs = lax.dot_general(g, vc, nt, preferred_element_type=jnp.float32)
        ds_low = (probs * (dprobs - delta)).astype(jnp.bfloat16)
        dq = jnp.dot(ds_low, kc, preferred_element_type=jnp.float32) * scale
        dq_ref[i * rows:(i + 1) * rows, :] = dq.astype(jnp.bfloat16)
        dk_slots = lax.dot_general(ds_low, q, tn, preferred_element_type=jnp.float32) * scale
        dv_slots = lax.dot_general(probs_low, g, tn, preferred_element_type=jnp.float32)
        for j in range(slots):
            @pl.when(lives[j] != 0)
            def _():
                window = pl.ds(offsets[j], BLOCK)
                dkv_ref[owners[j], 0, window, :] += dk_slots[j * BLOCK:(j + 1) * BLOCK, :]
                dkv_ref[owners[j], 1, window, :] += dv_slots[j * BLOCK:(j + 1) * BLOCK, :]


def block_grads(q_rows, g_rows, kv_parts, listed, live, steps=2):
    nblocks, slots = listed.shape
    rows = q_rows.shape[0] // nblocks * steps
    width = slots * BLOCK
    kernel = functools.partial(grads_kernel, slots, steps)
    whole = lambda b, *_: (0, 0, 0, 0)
    grid_spec = pltpu.PrefetchScalarGridSpec(
        num_scalar_prefetch=2,
        grid=(nblocks // steps,),
        in_specs=[
            pl.BlockSpec((rows, HD), lambda b, *_: (b, 0)),
            pl.BlockSpec((rows, HD), lambda b, *_: (b, 0)),
            pl.BlockSpec(kv_parts.shape, whole),
        ],
        out_specs=[
            pl.BlockSpec((rows, HD), lambda b, *_: (b, 0)),
            pl.BlockSpec(kv_parts.shape, whole),
        ],
        scratch_shapes=[
            pltpu.VMEM((width, HD), jnp.bfloat16),
            pltpu.VMEM((width, HD), jnp.bfloat16),
        ],
    )
    return pl.pallas_call(
        kernel,
        grid_spec=grid_spec,
        out_shape=[
            jax.ShapeDtypeStruct(q_rows.shape, jnp.bfloat16),
            jax.ShapeDtypeStruct(kv_parts.shape, jnp.float32),
        ],
        compiler_params=pltpu.CompilerParams(dimension_semantics=("arbitrary",)),
        cost_estimate=pl.CostEstimate(
            flops=12 * nblocks * (rows // steps) * width * HD,
            transcendentals=nblocks * (rows // steps) * width,
            bytes_accessed=6 * q_rows.size + 6 * kv_parts.size,
        ),
        interpret=INTERPRET,
    )(listed.reshape(-1), live.reshape(-1).astype(jnp.int32), q_rows, g_rows, kv_parts)


def body(queries, keys, values, out_grad, window_blocks, global_blocks, random_blocks):
    lanes = lax.axis_size("seq")
    tok = queries.shape[1]
    repeat = lanes // KV
    q_local = queries[0].reshape(tok, HEADS, HD)
    g_local = out_grad[0].reshape(tok, HEADS, HD)
    q_heads, g_heads = (
        lax.all_to_all(q_local, "seq", split_axis=1, concat_axis=0, tiled=True),
        lax.all_to_all(g_local, "seq", split_axis=1, concat_axis=0, tiled=True),
    )
    k_lead = keys[0].reshape(tok, KV, HD).transpose(1, 0, 2)
    v_lead = values[0].reshape(tok, KV, HD).transpose(1, 0, 2)
    kv_send = jnp.repeat(jnp.stack([k_lead, v_lead], axis=1), repeat, axis=0)
    kv_parts = lax.all_to_all(kv_send, "seq", split_axis=0, concat_axis=0, tiled=True)
    seqlen = q_heads.shape[0]
    per_device = q_heads.shape[1]
    listed, live = block_lists(window_blocks, global_blocks, random_blocks)
    q_rows = q_heads.reshape(seqlen * per_device, HD)
    g_rows = g_heads.reshape(seqlen * per_device, HD)
    dq_rows, dkv = block_grads(q_rows, g_rows, kv_parts, listed, live)
    dq_heads = dq_rows.reshape(seqlen, per_device, HD)
    dq_tokens = lax.all_to_all(dq_heads, "seq", split_axis=0, concat_axis=1, tiled=True)
    dkv_parts = lax.all_to_all(dkv, "seq", split_axis=0, concat_axis=0, tiled=True)
    dkv_sum = jnp.sum(dkv_parts.reshape(KV, repeat, 2, tok, HD), axis=1).astype(jnp.bfloat16)
    dk_tokens = dkv_sum[:, 0].transpose(1, 0, 2)
    dv_tokens = dkv_sum[:, 1].transpose(1, 0, 2)
    dq_flat = dq_tokens.reshape(1, tok, HEADS * HD)
    dk_flat = dk_tokens.reshape(1, tok, KV * HD)
    dv_flat = dv_tokens.reshape(1, tok, KV * HD)
    return from_behind((dq_flat, dk_flat, dv_flat), "pipe", -1)


def solution(mesh):
    in_specs = (
        P("pipe", "seq", None),
        P("pipe", "seq", None),
        P("pipe", "seq", None),
        P("pipe", "seq", None),
        P(),
        P(),
        P(),
    )
    out_specs = (P("pipe", "seq", None), P("pipe", "seq", None), P("pipe", "seq", None))
    return jax.shard_map(body, mesh=mesh, in_specs=in_specs, out_specs=out_specs, check_vma=False)
```

```python
import functools

import jax
import jax.numpy as jnp
from jax import lax
from jax.experimental import pallas as pl
from jax.experimental.pallas import tpu as pltpu
from jax.sharding import PartitionSpec as P

HEADS = 64
KV = 8
HD = 128
BLOCK = 64
INTERPRET = False


def from_behind(block, axis, distance):
    devices = range(lax.axis_size(axis))
    route = [(i - distance, i) for i in devices if i - distance in devices]
    return lax.ppermute(block, axis, route)


def block_lists(window_blocks, global_blocks, random_blocks):
    listed = jnp.concatenate([window_blocks, global_blocks, random_blocks], axis=1)
    width = listed.shape[1]
    same = listed[:, :, None] == listed[:, None, :]
    earlier = jnp.arange(width)[None, :] < jnp.arange(width)[:, None]
    repeated = jnp.any(jnp.logical_and(same, earlier[None]), axis=2)
    return (listed, jnp.logical_not(repeated))


def grads_kernel(slots, steps, listed_ref, live_ref, q_ref, g_ref, kv_ref, dq_ref, dkv_ref, kc_ref, vc_ref):
    b = pl.program_id(0)
    scale = HD ** (-0.5)
    width = slots * BLOCK
    half = kv_ref.shape[2] // BLOCK

    @pl.when(b == 0)
    def _():
        dkv_ref[...] = jnp.zeros(dkv_ref.shape, dkv_ref.dtype)

    col = lax.broadcasted_iota(jnp.int32, (1, width), 1)
    nt = (((1,), (1,)), ((), ()))
    tn = (((0,), (0,)), ((), ()))
    for i in range(steps):
        base = (b * steps + i) * slots
        owners = []
        offsets = []
        lives = []
        for j in range(slots):
            n = listed_ref[base + j]
            owners.append(n // half)
            offsets.append(pl.multiple_of((n % half) * BLOCK, BLOCK))
            lives.append(live_ref[base + j])
            kc_ref[j * BLOCK:(j + 1) * BLOCK, :] = kv_ref[owners[j], 0, pl.ds(offsets[j], BLOCK), :]
            vc_ref[j * BLOCK:(j + 1) * BLOCK, :] = kv_ref[owners[j], 1, pl.ds(offsets[j], BLOCK), :]
        q = q_ref[:, i * BLOCK:(i + 1) * BLOCK, :].reshape(-1, HD)
        g = g_ref[:, i * BLOCK:(i + 1) * BLOCK, :].reshape(-1, HD)
        kc = kc_ref[...]
        vc = vc_ref[...]
        live_cols = jnp.zeros((1, width), jnp.int32)
        for j in range(slots):
            inside = jnp.logical_and(col >= j * BLOCK, col < (j + 1) * BLOCK)
            live_cols = jnp.where(inside, lives[j], live_cols)
        scores = lax.dot_general(q, kc, nt, preferred_element_type=jnp.float32) * scale
        scores = jnp.where(live_cols != 0, scores, -jnp.inf)
        top = jnp.max(scores, axis=-1, keepdims=True)
        expd = jnp.exp(scores - top)
        probs = expd / jnp.sum(expd, axis=-1, keepdims=True)
        probs_low = probs.astype(jnp.bfloat16)
        attn = jnp.dot(probs_low, vc, preferred_element_type=jnp.float32)
        attn = attn.astype(jnp.bfloat16).astype(jnp.float32)
        delta = jnp.sum(g.astype(jnp.float32) * attn, axis=-1, keepdims=True)
        dprobs = lax.dot_general(g, vc, nt, preferred_element_type=jnp.float32)
        ds_low = (probs * (dprobs - delta)).astype(jnp.bfloat16)
        dq = jnp.dot(ds_low, kc, preferred_element_type=jnp.float32) * scale
        dq_ref[:, i * BLOCK:(i + 1) * BLOCK, :] = dq.astype(jnp.bfloat16).reshape(-1, BLOCK, HD)
        dk_slots = lax.dot_general(ds_low, q, tn, preferred_element_type=jnp.float32) * scale
        dv_slots = lax.dot_general(probs_low, g, tn, preferred_element_type=jnp.float32)
        for j in range(slots):
            @pl.when(lives[j] != 0)
            def _():
                window = pl.ds(offsets[j], BLOCK)
                dkv_ref[owners[j], 0, window, :] += dk_slots[j * BLOCK:(j + 1) * BLOCK, :]
                dkv_ref[owners[j], 1, window, :] += dv_slots[j * BLOCK:(j + 1) * BLOCK, :]


def block_grads(packed, listed, live, steps=2):
    nblocks, slots = listed.shape
    lanes, _, tok, _ = packed.shape
    half = tok // BLOCK
    per_device = 2
    rows = BLOCK * steps
    width = slots * BLOCK
    kernel = functools.partial(grads_kernel, slots, steps)
    grid_spec = pltpu.PrefetchScalarGridSpec(
        num_scalar_prefetch=2,
        grid=(nblocks // steps,),
        in_specs=[
            pl.BlockSpec((None, per_device, rows, HD), lambda b, *_: (b * steps // half, 0, b % (half // steps), 0)),
            pl.BlockSpec((None, per_device, rows, HD), lambda b, *_: (b * steps // half, 1, b % (half // steps), 0)),
            pl.BlockSpec((lanes, 2, tok, HD), lambda b, *_: (0, 2, 0, 0)),
        ],
        out_specs=[
            pl.BlockSpec((None, per_device, rows, HD), lambda b, *_: (b * steps // half, 0, b % (half // steps), 0)),
            pl.BlockSpec((lanes, 2, tok, HD), lambda b, *_: (0, 0, 0, 0)),
        ],
        scratch_shapes=[
            pltpu.VMEM((width, HD), jnp.bfloat16),
            pltpu.VMEM((width, HD), jnp.bfloat16),
        ],
    )
    return pl.pallas_call(
        kernel,
        grid_spec=grid_spec,
        out_shape=[
            jax.ShapeDtypeStruct((lanes, per_device, tok, HD), jnp.bfloat16),
            jax.ShapeDtypeStruct((lanes, 2, tok, HD), jnp.float32),
        ],
        compiler_params=pltpu.CompilerParams(dimension_semantics=("arbitrary",)),
        cost_estimate=pl.CostEstimate(
            flops=12 * nblocks * BLOCK * per_device * width * HD,
            transcendentals=nblocks * BLOCK * per_device * width,
            bytes_accessed=6 * packed.size,
        ),
        interpret=INTERPRET,
    )(listed.reshape(-1), live.reshape(-1).astype(jnp.int32), packed, packed, packed)


def body(queries, keys, values, out_grad, window_blocks, global_blocks, random_blocks):
    lanes = lax.axis_size("seq")
    tok = queries.shape[1]
    repeat = lanes // KV
    per_device = HEADS // lanes
    q_lead = queries[0].reshape(tok, lanes, per_device, HD).transpose(1, 2, 0, 3)
    g_lead = out_grad[0].reshape(tok, lanes, per_device, HD).transpose(1, 2, 0, 3)
    k_lead = jnp.repeat(keys[0].reshape(tok, KV, 1, HD).transpose(1, 2, 0, 3), repeat, axis=0)
    v_lead = jnp.repeat(values[0].reshape(tok, KV, 1, HD).transpose(1, 2, 0, 3), repeat, axis=0)
    send = jnp.concatenate([q_lead, g_lead, k_lead, v_lead], axis=1)
    packed = lax.all_to_all(send, "seq", split_axis=0, concat_axis=0, tiled=True)
    listed, live = block_lists(window_blocks, global_blocks, random_blocks)
    dq_heads, dkv = block_grads(packed, listed, live)
    dq_parts = lax.all_to_all(dq_heads, "seq", split_axis=0, concat_axis=0, tiled=True)
    dq_tokens = dq_parts.transpose(2, 0, 1, 3)
    dkv_parts = lax.all_to_all(dkv, "seq", split_axis=0, concat_axis=0, tiled=True)
    dkv_sum = jnp.sum(dkv_parts.reshape(KV, repeat, 2, tok, HD), axis=1).astype(jnp.bfloat16)
    dk_tokens = dkv_sum[:, 0].transpose(1, 0, 2)
    dv_tokens = dkv_sum[:, 1].transpose(1, 0, 2)
    dq_flat = dq_tokens.reshape(1, tok, HEADS * HD)
    dk_flat = dk_tokens.reshape(1, tok, KV * HD)
    dv_flat = dv_tokens.reshape(1, tok, KV * HD)
    return from_behind((dq_flat, dk_flat, dv_flat), "pipe", -1)


def solution(mesh):
    in_specs = (
        P("pipe", "seq", None),
        P("pipe", "seq", None),
        P("pipe", "seq", None),
        P("pipe", "seq", None),
        P(),
        P(),
        P(),
    )
    out_specs = (P("pipe", "seq", None), P("pipe", "seq", None), P("pipe", "seq", None))
    return jax.shard_map(body, mesh=mesh, in_specs=in_specs, out_specs=out_specs, check_vma=False)
```

```python
import functools

import jax
import jax.numpy as jnp
from jax import lax
from jax.experimental import pallas as pl
from jax.experimental.pallas import tpu as pltpu
from jax.sharding import PartitionSpec as P

HEADS = 64
KV = 8
HD = 128
BLOCK = 64
INTERPRET = False


def from_behind(block, axis, distance):
    devices = range(lax.axis_size(axis))
    route = [(i - distance, i) for i in devices if i - distance in devices]
    return lax.ppermute(block, axis, route)


def block_lists(window_blocks, global_blocks, random_blocks):
    listed = jnp.concatenate([window_blocks, global_blocks, random_blocks], axis=1)
    width = listed.shape[1]
    same = listed[:, :, None] == listed[:, None, :]
    earlier = jnp.arange(width)[None, :] < jnp.arange(width)[:, None]
    repeated = jnp.any(jnp.logical_and(same, earlier[None]), axis=2)
    return (listed, jnp.logical_not(repeated))


def grads_kernel(slots, steps, listed_ref, live_ref, q_ref, g_ref, kv_ref, dq_ref, dkv_ref, kc_ref, vc_ref):
    b = pl.program_id(0)
    scale = HD ** (-0.5)
    width = slots * BLOCK
    half = kv_ref.shape[2] // BLOCK

    @pl.when(b == 0)
    def _():
        dkv_ref[...] = jnp.zeros(dkv_ref.shape, dkv_ref.dtype)

    col = lax.broadcasted_iota(jnp.int32, (1, width), 1)
    nt = (((1,), (1,)), ((), ()))
    tn = (((0,), (0,)), ((), ()))
    for i in range(steps):
        base = (b * steps + i) * slots
        owners = []
        offsets = []
        lives = []
        for j in range(slots):
            n = listed_ref[base + j]
            owners.append(n // half)
            offsets.append(pl.multiple_of((n % half) * BLOCK, BLOCK))
            lives.append(live_ref[base + j])
            kc_ref[j * BLOCK:(j + 1) * BLOCK, :] = kv_ref[owners[j], 0, pl.ds(offsets[j], BLOCK), :]
            vc_ref[j * BLOCK:(j + 1) * BLOCK, :] = kv_ref[owners[j], 1, pl.ds(offsets[j], BLOCK), :]
        owner, within = divmod(i, half)
        q = q_ref[owner, :, within * BLOCK:(within + 1) * BLOCK, :].reshape(-1, HD)
        g = g_ref[owner, :, within * BLOCK:(within + 1) * BLOCK, :].reshape(-1, HD)
        kc = kc_ref[...]
        vc = vc_ref[...]
        live_cols = jnp.zeros((1, width), jnp.int32)
        for j in range(slots):
            inside = jnp.logical_and(col >= j * BLOCK, col < (j + 1) * BLOCK)
            live_cols = jnp.where(inside, lives[j], live_cols)
        scores = lax.dot_general(q, kc, nt, preferred_element_type=jnp.float32) * scale
        scores = jnp.where(live_cols != 0, scores, -jnp.inf)
        top = jnp.max(scores, axis=-1, keepdims=True)
        expd = jnp.exp(scores - top)
        probs = expd / jnp.sum(expd, axis=-1, keepdims=True)
        probs_low = probs.astype(jnp.bfloat16)
        attn = jnp.dot(probs_low, vc, preferred_element_type=jnp.float32)
        attn = attn.astype(jnp.bfloat16).astype(jnp.float32)
        delta = jnp.sum(g.astype(jnp.float32) * attn, axis=-1, keepdims=True)
        dprobs = lax.dot_general(g, vc, nt, preferred_element_type=jnp.float32)
        ds_low = (probs * (dprobs - delta)).astype(jnp.bfloat16)
        dq = jnp.dot(ds_low, kc, preferred_element_type=jnp.float32) * scale
        dq_ref[owner, :, within * BLOCK:(within + 1) * BLOCK, :] = dq.astype(jnp.bfloat16).reshape(-1, BLOCK, HD)
        dk_slots = lax.dot_general(ds_low, q, tn, preferred_element_type=jnp.float32) * scale
        dv_slots = lax.dot_general(probs_low, g, tn, preferred_element_type=jnp.float32)
        for j in range(slots):
            @pl.when(lives[j] != 0)
            def _():
                window = pl.ds(offsets[j], BLOCK)
                dkv_ref[owners[j], 0, window, :] += dk_slots[j * BLOCK:(j + 1) * BLOCK, :]
                dkv_ref[owners[j], 1, window, :] += dv_slots[j * BLOCK:(j + 1) * BLOCK, :]


def block_grads(packed, listed, live, steps=4):
    nblocks, slots = listed.shape
    lanes, _, tok, _ = packed.shape
    half = tok // BLOCK
    per_device = 2
    group = steps // half
    width = slots * BLOCK
    kernel = functools.partial(grads_kernel, slots, steps)
    grid_spec = pltpu.PrefetchScalarGridSpec(
        num_scalar_prefetch=2,
        grid=(nblocks // steps,),
        in_specs=[
            pl.BlockSpec((group, per_device, tok, HD), lambda b, *_: (b, 0, 0, 0)),
            pl.BlockSpec((group, per_device, tok, HD), lambda b, *_: (b, 1, 0, 0)),
            pl.BlockSpec((lanes, 2, tok, HD), lambda b, *_: (0, 2, 0, 0)),
        ],
        out_specs=[
            pl.BlockSpec((group, per_device, tok, HD), lambda b, *_: (b, 0, 0, 0)),
            pl.BlockSpec((lanes, 2, tok, HD), lambda b, *_: (0, 0, 0, 0)),
        ],
        scratch_shapes=[
            pltpu.VMEM((width, HD), jnp.bfloat16),
            pltpu.VMEM((width, HD), jnp.bfloat16),
        ],
    )
    return pl.pallas_call(
        kernel,
        grid_spec=grid_spec,
        out_shape=[
            jax.ShapeDtypeStruct((lanes, per_device, tok, HD), jnp.bfloat16),
            jax.ShapeDtypeStruct((lanes, 2, tok, HD), jnp.float32),
        ],
        compiler_params=pltpu.CompilerParams(dimension_semantics=("arbitrary",)),
        cost_estimate=pl.CostEstimate(
            flops=12 * nblocks * BLOCK * per_device * width * HD,
            transcendentals=nblocks * BLOCK * per_device * width,
            bytes_accessed=6 * packed.size,
        ),
        interpret=INTERPRET,
    )(listed.reshape(-1), live.reshape(-1).astype(jnp.int32), packed, packed, packed)


def body(queries, keys, values, out_grad, window_blocks, global_blocks, random_blocks):
    lanes = lax.axis_size("seq")
    tok = queries.shape[1]
    repeat = lanes // KV
    per_device = HEADS // lanes
    q_lead = queries[0].reshape(tok, lanes, per_device, HD).transpose(1, 2, 0, 3)
    g_lead = out_grad[0].reshape(tok, lanes, per_device, HD).transpose(1, 2, 0, 3)
    k_lead = jnp.repeat(keys[0].reshape(tok, KV, 1, HD).transpose(1, 2, 0, 3), repeat, axis=0)
    v_lead = jnp.repeat(values[0].reshape(tok, KV, 1, HD).transpose(1, 2, 0, 3), repeat, axis=0)
    send = jnp.concatenate([q_lead, g_lead, k_lead, v_lead], axis=1)
    packed = lax.all_to_all(send, "seq", split_axis=0, concat_axis=0, tiled=True)
    listed, live = block_lists(window_blocks, global_blocks, random_blocks)
    dq_heads, dkv = block_grads(packed, listed, live)
    dq_parts = lax.all_to_all(dq_heads, "seq", split_axis=0, concat_axis=0, tiled=True)
    dq_tokens = dq_parts.transpose(2, 0, 1, 3)
    dkv_parts = lax.all_to_all(dkv, "seq", split_axis=0, concat_axis=0, tiled=True)
    dkv_sum = jnp.sum(dkv_parts.reshape(KV, repeat, 2, tok, HD), axis=1).astype(jnp.bfloat16)
    dk_tokens = dkv_sum[:, 0].transpose(1, 0, 2)
    dv_tokens = dkv_sum[:, 1].transpose(1, 0, 2)
    dq_flat = dq_tokens.reshape(1, tok, HEADS * HD)
    dk_flat = dk_tokens.reshape(1, tok, KV * HD)
    dv_flat = dv_tokens.reshape(1, tok, KV * HD)
    return from_behind((dq_flat, dk_flat, dv_flat), "pipe", -1)


def solution(mesh):
    in_specs = (
        P("pipe", "seq", None),
        P("pipe", "seq", None),
        P("pipe", "seq", None),
        P("pipe", "seq", None),
        P(),
        P(),
        P(),
    )
    out_specs = (P("pipe", "seq", None), P("pipe", "seq", None), P("pipe", "seq", None))
    return jax.shard_map(body, mesh=mesh, in_specs=in_specs, out_specs=out_specs, check_vma=False)
```

```python
import functools

import jax
import jax.numpy as jnp
from jax import lax
from jax.experimental import pallas as pl
from jax.experimental.pallas import tpu as pltpu
from jax.sharding import PartitionSpec as P

HEADS = 64
KV = 8
HD = 128
BLOCK = 64
INTERPRET = False


def from_behind(block, axis, distance):
    devices = range(lax.axis_size(axis))
    route = [(i - distance, i) for i in devices if i - distance in devices]
    return lax.ppermute(block, axis, route)


def block_lists(window_blocks, global_blocks, random_blocks):
    listed = jnp.concatenate([window_blocks, global_blocks, random_blocks], axis=1)
    width = listed.shape[1]
    same = listed[:, :, None] == listed[:, None, :]
    earlier = jnp.arange(width)[None, :] < jnp.arange(width)[:, None]
    repeated = jnp.any(jnp.logical_and(same, earlier[None]), axis=2)
    return (listed, jnp.logical_not(repeated))


def grads_kernel(slots, steps, listed_ref, live_ref, q_ref, g_ref, kv_ref, dq_ref, out_ref, kc_ref, vc_ref, dkv_ref):
    b = pl.program_id(0)
    scale = HD ** (-0.5)
    width = slots * BLOCK
    half = kv_ref.shape[2] // BLOCK

    @pl.when(b == 0)
    def _():
        dkv_ref[...] = jnp.zeros(dkv_ref.shape, dkv_ref.dtype)

    col = lax.broadcasted_iota(jnp.int32, (1, width), 1)
    nt = (((1,), (1,)), ((), ()))
    tn = (((0,), (0,)), ((), ()))
    for i in range(steps):
        base = (b * steps + i) * slots
        owners = []
        offsets = []
        lives = []
        for j in range(slots):
            n = listed_ref[base + j]
            owners.append(n // half)
            offsets.append(pl.multiple_of((n % half) * BLOCK, BLOCK))
            lives.append(live_ref[base + j])
            kc_ref[j * BLOCK:(j + 1) * BLOCK, :] = kv_ref[owners[j], 0, pl.ds(offsets[j], BLOCK), :]
            vc_ref[j * BLOCK:(j + 1) * BLOCK, :] = kv_ref[owners[j], 1, pl.ds(offsets[j], BLOCK), :]
        owner, within = divmod(i, half)
        q = q_ref[owner, :, within * BLOCK:(within + 1) * BLOCK, :].reshape(-1, HD)
        g = g_ref[owner, :, within * BLOCK:(within + 1) * BLOCK, :].reshape(-1, HD)
        kc = kc_ref[...]
        vc = vc_ref[...]
        live_cols = jnp.zeros((1, width), jnp.int32)
        for j in range(slots):
            inside = jnp.logical_and(col >= j * BLOCK, col < (j + 1) * BLOCK)
            live_cols = jnp.where(inside, lives[j], live_cols)
        scores = lax.dot_general(q, kc, nt, preferred_element_type=jnp.float32) * scale
        scores = jnp.where(live_cols != 0, scores, -jnp.inf)
        top = jnp.max(scores, axis=-1, keepdims=True)
        expd = jnp.exp(scores - top)
        probs = expd / jnp.sum(expd, axis=-1, keepdims=True)
        probs_low = probs.astype(jnp.bfloat16)
        attn = jnp.dot(probs_low, vc, preferred_element_type=jnp.float32)
        attn = attn.astype(jnp.bfloat16).astype(jnp.float32)
        delta = jnp.sum(g.astype(jnp.float32) * attn, axis=-1, keepdims=True)
        dprobs = lax.dot_general(g, vc, nt, preferred_element_type=jnp.float32)
        ds_low = (probs * (dprobs - delta)).astype(jnp.bfloat16)
        dq = jnp.dot(ds_low, kc, preferred_element_type=jnp.float32) * scale
        dq_ref[owner, :, within * BLOCK:(within + 1) * BLOCK, :] = dq.astype(jnp.bfloat16).reshape(-1, BLOCK, HD)
        dk_slots = lax.dot_general(ds_low, q, tn, preferred_element_type=jnp.float32) * scale
        dv_slots = lax.dot_general(probs_low, g, tn, preferred_element_type=jnp.float32)
        for j in range(slots):
            @pl.when(lives[j] != 0)
            def _():
                window = pl.ds(offsets[j], BLOCK)
                dkv_ref[owners[j], 0, window, :] += dk_slots[j * BLOCK:(j + 1) * BLOCK, :]
                dkv_ref[owners[j], 1, window, :] += dv_slots[j * BLOCK:(j + 1) * BLOCK, :]

    @pl.when(b == pl.num_programs(0) - 1)
    def _():
        out_ref[...] = dkv_ref[...].astype(out_ref.dtype)


def block_grads(packed, listed, live, steps=4):
    nblocks, slots = listed.shape
    lanes, _, tok, _ = packed.shape
    half = tok // BLOCK
    per_device = 2
    group = steps // half
    width = slots * BLOCK
    kernel = functools.partial(grads_kernel, slots, steps)
    grid_spec = pltpu.PrefetchScalarGridSpec(
        num_scalar_prefetch=2,
        grid=(nblocks // steps,),
        in_specs=[
            pl.BlockSpec((group, per_device, tok, HD), lambda b, *_: (b, 0, 0, 0)),
            pl.BlockSpec((group, per_device, tok, HD), lambda b, *_: (b, 1, 0, 0)),
            pl.BlockSpec((lanes, 2, tok, HD), lambda b, *_: (0, 2, 0, 0)),
        ],
        out_specs=[
            pl.BlockSpec((group, per_device, tok, HD), lambda b, *_: (b, 0, 0, 0)),
            pl.BlockSpec((lanes, 2, tok, HD), lambda b, *_: (0, 0, 0, 0)),
        ],
        scratch_shapes=[
            pltpu.VMEM((width, HD), jnp.bfloat16),
            pltpu.VMEM((width, HD), jnp.bfloat16),
            pltpu.VMEM((lanes, 2, tok, HD), jnp.float32),
        ],
    )
    return pl.pallas_call(
        kernel,
        grid_spec=grid_spec,
        out_shape=[
            jax.ShapeDtypeStruct((lanes, per_device, tok, HD), jnp.bfloat16),
            jax.ShapeDtypeStruct((lanes, 2, tok, HD), jnp.bfloat16),
        ],
        compiler_params=pltpu.CompilerParams(dimension_semantics=("arbitrary",)),
        cost_estimate=pl.CostEstimate(
            flops=12 * nblocks * BLOCK * per_device * width * HD,
            transcendentals=nblocks * BLOCK * per_device * width,
            bytes_accessed=6 * packed.size,
        ),
        interpret=INTERPRET,
    )(listed.reshape(-1), live.reshape(-1).astype(jnp.int32), packed, packed, packed)


def body(queries, keys, values, out_grad, window_blocks, global_blocks, random_blocks):
    lanes = lax.axis_size("seq")
    tok = queries.shape[1]
    repeat = lanes // KV
    per_device = HEADS // lanes
    q_lead = queries[0].reshape(tok, lanes, per_device, HD).transpose(1, 2, 0, 3)
    g_lead = out_grad[0].reshape(tok, lanes, per_device, HD).transpose(1, 2, 0, 3)
    k_lead = jnp.repeat(keys[0].reshape(tok, KV, 1, HD).transpose(1, 2, 0, 3), repeat, axis=0)
    v_lead = jnp.repeat(values[0].reshape(tok, KV, 1, HD).transpose(1, 2, 0, 3), repeat, axis=0)
    send = jnp.concatenate([q_lead, g_lead, k_lead, v_lead], axis=1)
    packed = lax.all_to_all(send, "seq", split_axis=0, concat_axis=0, tiled=True)
    listed, live = block_lists(window_blocks, global_blocks, random_blocks)
    dq_heads, dkv = block_grads(packed, listed, live)
    dq_parts = lax.all_to_all(dq_heads, "seq", split_axis=0, concat_axis=0, tiled=True)
    dq_tokens = dq_parts.transpose(2, 0, 1, 3)
    dkv_parts = lax.all_to_all(dkv, "seq", split_axis=0, concat_axis=0, tiled=True)
    dkv_wide = dkv_parts.reshape(KV, repeat, 2, tok, HD).astype(jnp.float32)
    dkv_sum = jnp.sum(dkv_wide, axis=1).astype(jnp.bfloat16)
    dk_tokens = dkv_sum[:, 0].transpose(1, 0, 2)
    dv_tokens = dkv_sum[:, 1].transpose(1, 0, 2)
    dq_flat = dq_tokens.reshape(1, tok, HEADS * HD)
    dk_flat = dk_tokens.reshape(1, tok, KV * HD)
    dv_flat = dv_tokens.reshape(1, tok, KV * HD)
    return from_behind((dq_flat, dk_flat, dv_flat), "pipe", -1)


def solution(mesh):
    in_specs = (
        P("pipe", "seq", None),
        P("pipe", "seq", None),
        P("pipe", "seq", None),
        P("pipe", "seq", None),
        P(),
        P(),
        P(),
    )
    out_specs = (P("pipe", "seq", None), P("pipe", "seq", None), P("pipe", "seq", None))
    return jax.shard_map(body, mesh=mesh, in_specs=in_specs, out_specs=out_specs, check_vma=False)
```

```python
import functools

import jax
import jax.numpy as jnp
from jax import lax
from jax.experimental import pallas as pl
from jax.experimental.pallas import tpu as pltpu
from jax.sharding import PartitionSpec as P


HEADS = 64
KV = 8
HD = 128
BLOCK = 64
INTERPRET = False


def from_behind(block, axis, distance):
    devices = range(lax.axis_size(axis))
    route = [(i - distance, i) for i in devices if i - distance in devices]
    return lax.ppermute(block, axis, route)


def block_lists(window_blocks, global_blocks, random_blocks):
    listed = jnp.concatenate([window_blocks, global_blocks, random_blocks], axis=1)
    width = listed.shape[1]
    same = listed[:, :, None] == listed[:, None, :]
    earlier = jnp.arange(width)[None, :] < jnp.arange(width)[:, None]
    repeated = jnp.any(jnp.logical_and(same, earlier[None]), axis=2)
    return (listed, jnp.logical_not(repeated))


def grads_kernel(slots, steps, part, chained, listed_ref, live_ref, q_ref, g_ref, kv_ref, *refs):
    if chained:
        acc_in_ref, dq_ref, out_ref, kc_ref, vc_ref, dkv_ref = refs
    else:
        dq_ref, out_ref, kc_ref, vc_ref, dkv_ref = refs
    b = pl.program_id(0)
    scale = HD ** (-0.5)
    width = slots * BLOCK
    half = kv_ref.shape[2] // BLOCK

    @pl.when(b == 0)
    def _():
        if chained:
            dkv_ref[...] = acc_in_ref[...]
        else:
            dkv_ref[...] = jnp.zeros(dkv_ref.shape, dkv_ref.dtype)

    col = lax.broadcasted_iota(jnp.int32, (1, width), 1)
    nt = (((1,), (1,)), ((), ()))
    tn = (((0,), (0,)), ((), ()))
    for i in range(steps):
        base = ((b * steps + i) * half + part) * slots
        owners = []
        offsets = []
        lives = []
        for j in range(slots):
            n = listed_ref[base + j]
            owners.append(n // half)
            offsets.append(pl.multiple_of((n % half) * BLOCK, BLOCK))
            lives.append(live_ref[base + j])
            kc_ref[j * BLOCK:(j + 1) * BLOCK, :] = kv_ref[owners[j], 0, pl.ds(offsets[j], BLOCK), :]
            vc_ref[j * BLOCK:(j + 1) * BLOCK, :] = kv_ref[owners[j], 1, pl.ds(offsets[j], BLOCK), :]
        q = q_ref[i].reshape(-1, HD)
        g = g_ref[i].reshape(-1, HD)
        kc = kc_ref[...]
        vc = vc_ref[...]
        live_cols = jnp.zeros((1, width), jnp.int32)
        for j in range(slots):
            inside = jnp.logical_and(col >= j * BLOCK, col < (j + 1) * BLOCK)
            live_cols = jnp.where(inside, lives[j], live_cols)
        scores = lax.dot_general(q, kc, nt, preferred_element_type=jnp.float32) * scale
        scores = jnp.where(live_cols != 0, scores, -jnp.inf)
        top = jnp.max(scores, axis=-1, keepdims=True)
        expd = jnp.exp(scores - top)
        probs = expd / jnp.sum(expd, axis=-1, keepdims=True)
        probs_low = probs.astype(jnp.bfloat16)
        attn = jnp.dot(probs_low, vc, preferred_element_type=jnp.float32)
        attn = attn.astype(jnp.bfloat16).astype(jnp.float32)
        delta = jnp.sum(g.astype(jnp.float32) * attn, axis=-1, keepdims=True)
        dprobs = lax.dot_general(g, vc, nt, preferred_element_type=jnp.float32)
        ds_low = (probs * (dprobs - delta)).astype(jnp.bfloat16)
        dq = jnp.dot(ds_low, kc, preferred_element_type=jnp.float32) * scale
        dq_ref[i] = dq.astype(jnp.bfloat16).reshape(dq_ref.shape[1:])
        dk_slots = lax.dot_general(ds_low, q, tn, preferred_element_type=jnp.float32) * scale
        dv_slots = lax.dot_general(probs_low, g, tn, preferred_element_type=jnp.float32)
        for j in range(slots):
            @pl.when(lives[j] != 0)
            def _():
                window = pl.ds(offsets[j], BLOCK)
                dkv_ref[owners[j], 0, window, :] += dk_slots[j * BLOCK:(j + 1) * BLOCK, :]
                dkv_ref[owners[j], 1, window, :] += dv_slots[j * BLOCK:(j + 1) * BLOCK, :]

    @pl.when(b == pl.num_programs(0) - 1)
    def _():
        out_ref[...] = dkv_ref[...].astype(out_ref.dtype)


def block_grads(packed, listed, live, part, acc_in=None, out_dtype=jnp.float32, steps=4):
    nblocks, slots = listed.shape
    lanes, _, tok, _ = packed.shape
    per_device = 2
    width = slots * BLOCK
    chained = acc_in is not None
    kernel = functools.partial(grads_kernel, slots, steps, part, chained)
    whole = lambda b, *_: (0, 0, 0, 0)
    in_specs = [
        pl.BlockSpec((steps, per_device, BLOCK, HD), lambda b, *_: (b, 0, part, 0)),
        pl.BlockSpec((steps, per_device, BLOCK, HD), lambda b, *_: (b, 1, part, 0)),
        pl.BlockSpec((lanes, 2, tok, HD), lambda b, *_: (0, 2, 0, 0)),
    ]
    operands = [packed, packed, packed]
    if chained:
        in_specs.append(pl.BlockSpec((lanes, 2, tok, HD), whole))
        operands.append(acc_in)
    grid_spec = pltpu.PrefetchScalarGridSpec(
        num_scalar_prefetch=2,
        grid=(lanes // steps,),
        in_specs=in_specs,
        out_specs=[
            pl.BlockSpec((steps, per_device, BLOCK, HD), lambda b, *_: (b, 0, 0, 0)),
            pl.BlockSpec((lanes, 2, tok, HD), whole),
        ],
        scratch_shapes=[
            pltpu.VMEM((width, HD), jnp.bfloat16),
            pltpu.VMEM((width, HD), jnp.bfloat16),
            pltpu.VMEM((lanes, 2, tok, HD), jnp.float32),
        ],
    )
    return pl.pallas_call(
        kernel,
        grid_spec=grid_spec,
        out_shape=[
            jax.ShapeDtypeStruct((lanes, per_device, BLOCK, HD), jnp.bfloat16),
            jax.ShapeDtypeStruct((lanes, 2, tok, HD), out_dtype),
        ],
        compiler_params=pltpu.CompilerParams(dimension_semantics=("arbitrary",)),
        cost_estimate=pl.CostEstimate(
            flops=6 * nblocks * BLOCK * per_device * width * HD,
            transcendentals=nblocks * BLOCK * per_device * width // 2,
            bytes_accessed=3 * packed.size,
        ),
        interpret=INTERPRET,
    )(listed.reshape(-1), live.reshape(-1).astype(jnp.int32), *operands)


def body(queries, keys, values, out_grad, window_blocks, global_blocks, random_blocks):
    lanes = lax.axis_size("seq")
    tok = queries.shape[1]
    repeat = lanes // KV
    per_device = HEADS // lanes
    q_lead = queries[0].reshape(tok, lanes, per_device, HD).transpose(1, 2, 0, 3)
    g_lead = out_grad[0].reshape(tok, lanes, per_device, HD).transpose(1, 2, 0, 3)
    k_lead = jnp.repeat(keys[0].reshape(tok, KV, 1, HD).transpose(1, 2, 0, 3), repeat, axis=0)
    v_lead = jnp.repeat(values[0].reshape(tok, KV, 1, HD).transpose(1, 2, 0, 3), repeat, axis=0)
    send = jnp.concatenate([q_lead, g_lead, k_lead, v_lead], axis=1)
    packed = lax.all_to_all(send, "seq", split_axis=0, concat_axis=0, tiled=True)
    listed, live = block_lists(window_blocks, global_blocks, random_blocks)
    dq_first, acc = block_grads(packed, listed, live, 0)
    dq_first_next = from_behind(dq_first, "pipe", -1)
    dq_second, dkv = block_grads(packed, listed, live, 1, acc, jnp.bfloat16)
    dq_second_next = from_behind(dq_second, "pipe", -1)
    dkv_parts = lax.all_to_all(dkv, "seq", split_axis=0, concat_axis=0, tiled=True)
    dkv_wide = dkv_parts.reshape(KV, repeat, 2, tok, HD).astype(jnp.float32)
    dkv_sum = jnp.sum(dkv_wide, axis=1).astype(jnp.bfloat16)
    dk_tokens = dkv_sum[:, 0].transpose(1, 0, 2)
    dv_tokens = dkv_sum[:, 1].transpose(1, 0, 2)
    dk_flat = dk_tokens.reshape(1, tok, KV * HD)
    dv_flat = dv_tokens.reshape(1, tok, KV * HD)
    dk_next, dv_next = from_behind((dk_flat, dv_flat), "pipe", -1)
    dq_heads = jnp.concatenate([dq_first_next, dq_second_next], axis=2)
    dq_parts = lax.all_to_all(dq_heads, "seq", split_axis=0, concat_axis=0, tiled=True)
    dq_next = dq_parts.transpose(2, 0, 1, 3).reshape(1, tok, HEADS * HD)
    return dq_next, dk_next, dv_next


def solution(mesh):
    in_specs = (
        P("pipe", "seq", None),
        P("pipe", "seq", None),
        P("pipe", "seq", None),
        P("pipe", "seq", None),
        P(),
        P(),
        P(),
    )
    out_specs = (P("pipe", "seq", None), P("pipe", "seq", None), P("pipe", "seq", None))

    return jax.shard_map(body, mesh=mesh, in_specs=in_specs, out_specs=out_specs, check_vma=False)
```

```python
import functools

import jax
import jax.numpy as jnp
from jax import lax
from jax.experimental import pallas as pl
from jax.experimental.pallas import tpu as pltpu
from jax.sharding import PartitionSpec as P


HEADS = 64
KV = 8
HD = 128
BLOCK = 64
INTERPRET = False


def from_behind(block, axis, distance):
    devices = range(lax.axis_size(axis))
    route = [(i - distance, i) for i in devices if i - distance in devices]
    return lax.ppermute(block, axis, route)


def block_lists(window_blocks, global_blocks, random_blocks):
    listed = jnp.concatenate([window_blocks, global_blocks, random_blocks], axis=1)
    width = listed.shape[1]
    same = listed[:, :, None] == listed[:, None, :]
    earlier = jnp.arange(width)[None, :] < jnp.arange(width)[:, None]
    repeated = jnp.any(jnp.logical_and(same, earlier[None]), axis=2)
    return (listed, jnp.logical_not(repeated))


def grads_kernel(slots, steps, part, chained, listed_ref, live_ref, q_ref, g_ref, kv_ref, *refs):
    if chained:
        acc_in_ref, dq_ref, out_ref, kc_ref, vc_ref, dkv_ref = refs
    else:
        dq_ref, out_ref, kc_ref, vc_ref, dkv_ref = refs
    b = pl.program_id(0)
    scale = HD ** (-0.5)
    width = slots * BLOCK
    half = kv_ref.shape[2] // BLOCK

    @pl.when(b == 0)
    def _():
        if chained:
            dkv_ref[...] = acc_in_ref[...]
        else:
            dkv_ref[...] = jnp.zeros(dkv_ref.shape, dkv_ref.dtype)

    col = lax.broadcasted_iota(jnp.int32, (1, width), 1)
    nt = (((1,), (1,)), ((), ()))
    tn = (((0,), (0,)), ((), ()))
    for i in range(steps):
        base = ((b * steps + i) * half + part) * slots
        owners = []
        offsets = []
        lives = []
        for j in range(slots):
            n = listed_ref[base + j]
            owners.append(n // half)
            offsets.append(pl.multiple_of((n % half) * BLOCK, BLOCK))
            lives.append(live_ref[base + j])
            kc_ref[j * BLOCK:(j + 1) * BLOCK, :] = kv_ref[owners[j], 0, pl.ds(offsets[j], BLOCK), :]
            vc_ref[j * BLOCK:(j + 1) * BLOCK, :] = kv_ref[owners[j], 1, pl.ds(offsets[j], BLOCK), :]
        q = q_ref[i].reshape(-1, HD)
        g = g_ref[i].reshape(-1, HD)
        kc = kc_ref[...]
        vc = vc_ref[...]
        live_cols = jnp.zeros((1, width), jnp.int32)
        for j in range(slots):
            inside = jnp.logical_and(col >= j * BLOCK, col < (j + 1) * BLOCK)
            live_cols = jnp.where(inside, lives[j], live_cols)
        scores = lax.dot_general(q, kc, nt, preferred_element_type=jnp.float32) * scale
        scores = jnp.where(live_cols != 0, scores, -jnp.inf)
        top = jnp.max(scores, axis=-1, keepdims=True)
        expd = jnp.exp(scores - top)
        probs = expd / jnp.sum(expd, axis=-1, keepdims=True)
        probs_low = probs.astype(jnp.bfloat16)
        attn = jnp.dot(probs_low, vc, preferred_element_type=jnp.float32)
        attn = attn.astype(jnp.bfloat16).astype(jnp.float32)
        delta = jnp.sum(g.astype(jnp.float32) * attn, axis=-1, keepdims=True)
        dprobs = lax.dot_general(g, vc, nt, preferred_element_type=jnp.float32)
        ds_low = (probs * (dprobs - delta)).astype(jnp.bfloat16)
        dq = jnp.dot(ds_low, kc, preferred_element_type=jnp.float32) * scale
        dq_ref[i] = dq.astype(jnp.bfloat16).reshape(dq_ref.shape[1:])
        dk_slots = lax.dot_general(ds_low, q, tn, preferred_element_type=jnp.float32) * scale
        dv_slots = lax.dot_general(probs_low, g, tn, preferred_element_type=jnp.float32)
        for j in range(slots):
            @pl.when(lives[j] != 0)
            def _():
                window = pl.ds(offsets[j], BLOCK)
                dkv_ref[owners[j], 0, window, :] += dk_slots[j * BLOCK:(j + 1) * BLOCK, :]
                dkv_ref[owners[j], 1, window, :] += dv_slots[j * BLOCK:(j + 1) * BLOCK, :]

    @pl.when(b == pl.num_programs(0) - 1)
    def _():
        out_ref[...] = dkv_ref[...].astype(out_ref.dtype)


def block_grads(packed, listed, live, part, acc_in=None, out_dtype=jnp.float32, steps=4):
    nblocks, slots = listed.shape
    lanes, _, tok, _ = packed.shape
    per_device = 2
    width = slots * BLOCK
    chained = acc_in is not None
    kernel = functools.partial(grads_kernel, slots, steps, part, chained)
    whole = lambda b, *_: (0, 0, 0, 0)
    in_specs = [
        pl.BlockSpec((steps, per_device, BLOCK, HD), lambda b, *_: (b, 0, part, 0)),
        pl.BlockSpec((steps, per_device, BLOCK, HD), lambda b, *_: (b, 1, part, 0)),
        pl.BlockSpec((lanes, 2, tok, HD), lambda b, *_: (0, 2, 0, 0)),
    ]
    operands = [packed, packed, packed]
    if chained:
        in_specs.append(pl.BlockSpec((lanes, 2, tok, HD), whole))
        operands.append(acc_in)
    grid_spec = pltpu.PrefetchScalarGridSpec(
        num_scalar_prefetch=2,
        grid=(lanes // steps,),
        in_specs=in_specs,
        out_specs=[
            pl.BlockSpec((steps, per_device, BLOCK, HD), lambda b, *_: (b, 0, 0, 0)),
            pl.BlockSpec((lanes, 2, tok, HD), whole),
        ],
        scratch_shapes=[
            pltpu.VMEM((width, HD), jnp.bfloat16),
            pltpu.VMEM((width, HD), jnp.bfloat16),
            pltpu.VMEM((lanes, 2, tok, HD), jnp.float32),
        ],
    )
    return pl.pallas_call(
        kernel,
        grid_spec=grid_spec,
        out_shape=[
            jax.ShapeDtypeStruct((lanes, per_device, BLOCK, HD), jnp.bfloat16),
            jax.ShapeDtypeStruct((lanes, 2, tok, HD), out_dtype),
        ],
        compiler_params=pltpu.CompilerParams(dimension_semantics=("arbitrary",)),
        cost_estimate=pl.CostEstimate(
            flops=6 * nblocks * BLOCK * per_device * width * HD,
            transcendentals=nblocks * BLOCK * per_device * width // 2,
            bytes_accessed=3 * packed.size,
        ),
        interpret=INTERPRET,
    )(listed.reshape(-1), live.reshape(-1).astype(jnp.int32), *operands)


def pack_kernel(q_ref, g_ref, k_ref, v_ref, out_ref):
    out_ref[0] = q_ref[:, :HD]
    out_ref[1] = q_ref[:, HD:]
    out_ref[2] = g_ref[:, :HD]
    out_ref[3] = g_ref[:, HD:]
    out_ref[4] = k_ref[...]
    out_ref[5] = v_ref[...]


def pack(queries, out_grad, keys, values, lanes):
    tok = queries.shape[1]
    repeat = lanes // KV
    wide = pl.BlockSpec((None, tok, 2 * HD), lambda d: (0, 0, d))
    narrow = pl.BlockSpec((None, tok, HD), lambda d: (0, 0, d // repeat))
    return pl.pallas_call(
        pack_kernel,
        grid=(lanes,),
        in_specs=[wide, wide, narrow, narrow],
        out_specs=pl.BlockSpec((None, 6, tok, HD), lambda d: (d, 0, 0, 0)),
        out_shape=jax.ShapeDtypeStruct((lanes, 6, tok, HD), queries.dtype),
        compiler_params=pltpu.CompilerParams(dimension_semantics=("arbitrary",)),
        interpret=INTERPRET,
    )(queries, out_grad, keys, values)


def body(queries, keys, values, out_grad, window_blocks, global_blocks, random_blocks):
    lanes = lax.axis_size("seq")
    tok = queries.shape[1]
    repeat = lanes // KV
    send = pack(queries, out_grad, keys, values, lanes)
    packed = lax.all_to_all(send, "seq", split_axis=0, concat_axis=0, tiled=True)
    listed, live = block_lists(window_blocks, global_blocks, random_blocks)
    dq_first, acc = block_grads(packed, listed, live, 0)
    dq_first_next = from_behind(dq_first, "pipe", -1)
    dq_second, dkv = block_grads(packed, listed, live, 1, acc, jnp.bfloat16)
    dq_second_next = from_behind(dq_second, "pipe", -1)
    dkv_parts = lax.all_to_all(dkv, "seq", split_axis=0, concat_axis=0, tiled=True)
    dkv_wide = dkv_parts.reshape(KV, repeat, 2, tok, HD).astype(jnp.float32)
    dkv_sum = jnp.sum(dkv_wide, axis=1).astype(jnp.bfloat16)
    dk_tokens = dkv_sum[:, 0].transpose(1, 0, 2)
    dv_tokens = dkv_sum[:, 1].transpose(1, 0, 2)
    dk_flat = dk_tokens.reshape(1, tok, KV * HD)
    dv_flat = dv_tokens.reshape(1, tok, KV * HD)
    dk_next, dv_next = from_behind((dk_flat, dv_flat), "pipe", -1)
    dq_heads = jnp.concatenate([dq_first_next, dq_second_next], axis=2)
    dq_parts = lax.all_to_all(dq_heads, "seq", split_axis=0, concat_axis=0, tiled=True)
    dq_next = dq_parts.transpose(2, 0, 1, 3).reshape(1, tok, HEADS * HD)
    return dq_next, dk_next, dv_next


def solution(mesh):
    in_specs = (
        P("pipe", "seq", None),
        P("pipe", "seq", None),
        P("pipe", "seq", None),
        P("pipe", "seq", None),
        P(),
        P(),
        P(),
    )
    out_specs = (P("pipe", "seq", None), P("pipe", "seq", None), P("pipe", "seq", None))

    return jax.shard_map(body, mesh=mesh, in_specs=in_specs, out_specs=out_specs, check_vma=False)
```

```python
import functools

import jax
import jax.numpy as jnp
from jax import lax
from jax.experimental import pallas as pl
from jax.experimental.pallas import tpu as pltpu
from jax.sharding import PartitionSpec as P


HEADS = 64
KV = 8
HD = 128
BLOCK = 64
INTERPRET = False


def from_behind(block, axis, distance):
    devices = range(lax.axis_size(axis))
    route = [(i - distance, i) for i in devices if i - distance in devices]
    return lax.ppermute(block, axis, route)


def block_lists(window_blocks, global_blocks, random_blocks):
    listed = jnp.concatenate([window_blocks, global_blocks, random_blocks], axis=1)
    width = listed.shape[1]
    same = listed[:, :, None] == listed[:, None, :]
    earlier = jnp.arange(width)[None, :] < jnp.arange(width)[:, None]
    repeated = jnp.any(jnp.logical_and(same, earlier[None]), axis=2)
    return (listed, jnp.logical_not(repeated))


def grads_kernel(slots, steps, part, chained, listed_ref, live_ref, q_ref, g_ref, kv_ref, *refs):
    if chained:
        acc_in_ref, dq_ref, out_ref, kc_ref, vc_ref, dkv_ref = refs
    else:
        dq_ref, out_ref, kc_ref, vc_ref, dkv_ref = refs
    b = pl.program_id(0)
    scale = HD ** (-0.5)
    width = slots * BLOCK
    half = kv_ref.shape[2] // BLOCK

    @pl.when(b == 0)
    def _():
        if chained:
            dkv_ref[...] = acc_in_ref[...]
        else:
            dkv_ref[...] = jnp.zeros(dkv_ref.shape, dkv_ref.dtype)

    col = lax.broadcasted_iota(jnp.int32, (1, width), 1)
    nt = (((1,), (1,)), ((), ()))
    tn = (((0,), (0,)), ((), ()))
    for i in range(steps):
        base = ((b * steps + i) * half + part) * slots
        owners = []
        offsets = []
        lives = []
        for j in range(slots):
            n = listed_ref[base + j]
            owners.append(n // half)
            offsets.append(pl.multiple_of((n % half) * BLOCK, BLOCK))
            lives.append(live_ref[base + j])
            kc_ref[j * BLOCK:(j + 1) * BLOCK, :] = kv_ref[owners[j], 0, pl.ds(offsets[j], BLOCK), :]
            vc_ref[j * BLOCK:(j + 1) * BLOCK, :] = kv_ref[owners[j], 1, pl.ds(offsets[j], BLOCK), :]
        q = q_ref[i].reshape(-1, HD)
        g = g_ref[i].reshape(-1, HD)
        kc = kc_ref[...]
        vc = vc_ref[...]
        live_cols = jnp.zeros((1, width), jnp.int32)
        for j in range(slots):
            inside = jnp.logical_and(col >= j * BLOCK, col < (j + 1) * BLOCK)
            live_cols = jnp.where(inside, lives[j], live_cols)
        scores = lax.dot_general(q, kc, nt, preferred_element_type=jnp.float32) * scale
        scores = jnp.where(live_cols != 0, scores, -jnp.inf)
        top = jnp.max(scores, axis=-1, keepdims=True)
        expd = jnp.exp(scores - top)
        probs = expd / jnp.sum(expd, axis=-1, keepdims=True)
        probs_low = probs.astype(jnp.bfloat16)
        attn = jnp.dot(probs_low, vc, preferred_element_type=jnp.float32)
        attn = attn.astype(jnp.bfloat16).astype(jnp.float32)
        delta = jnp.sum(g.astype(jnp.float32) * attn, axis=-1, keepdims=True)
        dprobs = lax.dot_general(g, vc, nt, preferred_element_type=jnp.float32)
        ds_low = (probs * (dprobs - delta)).astype(jnp.bfloat16)
        dq = jnp.dot(ds_low, kc, preferred_element_type=jnp.float32) * scale
        dq_ref[i] = dq.astype(jnp.bfloat16).reshape(dq_ref.shape[1:])
        dk_slots = lax.dot_general(ds_low, q, tn, preferred_element_type=jnp.float32) * scale
        dv_slots = lax.dot_general(probs_low, g, tn, preferred_element_type=jnp.float32)
        for j in range(slots):
            @pl.when(lives[j] != 0)
            def _():
                window = pl.ds(offsets[j], BLOCK)
                dkv_ref[owners[j], 0, window, :] += dk_slots[j * BLOCK:(j + 1) * BLOCK, :]
                dkv_ref[owners[j], 1, window, :] += dv_slots[j * BLOCK:(j + 1) * BLOCK, :]

    @pl.when(b == pl.num_programs(0) - 1)
    def _():
        out_ref[...] = dkv_ref[...].astype(out_ref.dtype)


def block_grads(packed, listed, live, part, acc_in=None, out_dtype=jnp.float32, steps=4):
    nblocks, slots = listed.shape
    lanes, _, tok, _ = packed.shape
    per_device = 2
    width = slots * BLOCK
    chained = acc_in is not None
    kernel = functools.partial(grads_kernel, slots, steps, part, chained)
    whole = lambda b, *_: (0, 0, 0, 0)
    in_specs = [
        pl.BlockSpec((steps, per_device, BLOCK, HD), lambda b, *_: (b, 0, part, 0)),
        pl.BlockSpec((steps, per_device, BLOCK, HD), lambda b, *_: (b, 1, part, 0)),
        pl.BlockSpec((lanes, 2, tok, HD), lambda b, *_: (0, 2, 0, 0)),
    ]
    operands = [packed, packed, packed]
    if chained:
        in_specs.append(pl.BlockSpec((lanes, 2, tok, HD), whole))
        operands.append(acc_in)
    grid_spec = pltpu.PrefetchScalarGridSpec(
        num_scalar_prefetch=2,
        grid=(lanes // steps,),
        in_specs=in_specs,
        out_specs=[
            pl.BlockSpec((steps, per_device, BLOCK, HD), lambda b, *_: (b, 0, 0, 0)),
            pl.BlockSpec((lanes, 2, tok, HD), whole),
        ],
        scratch_shapes=[
            pltpu.VMEM((width, HD), jnp.bfloat16),
            pltpu.VMEM((width, HD), jnp.bfloat16),
            pltpu.VMEM((lanes, 2, tok, HD), jnp.float32),
        ],
    )
    return pl.pallas_call(
        kernel,
        grid_spec=grid_spec,
        out_shape=[
            jax.ShapeDtypeStruct((lanes, per_device, BLOCK, HD), jnp.bfloat16),
            jax.ShapeDtypeStruct((lanes, 2, tok, HD), out_dtype),
        ],
        compiler_params=pltpu.CompilerParams(dimension_semantics=("arbitrary",)),
        cost_estimate=pl.CostEstimate(
            flops=6 * nblocks * BLOCK * per_device * width * HD,
            transcendentals=nblocks * BLOCK * per_device * width // 2,
            bytes_accessed=3 * packed.size,
        ),
        interpret=INTERPRET,
    )(listed.reshape(-1), live.reshape(-1).astype(jnp.int32), *operands)


def pack_kernel(count, repeat, q_ref, g_ref, k_ref, v_ref, out_ref):
    for d in range(count):
        lead = slice(2 * d * HD, 2 * d * HD + HD)
        rest = slice(2 * d * HD + HD, 2 * (d + 1) * HD)
        head = slice(d // repeat * HD, (d // repeat + 1) * HD)
        out_ref[d, 0] = q_ref[:, lead]
        out_ref[d, 1] = q_ref[:, rest]
        out_ref[d, 2] = g_ref[:, lead]
        out_ref[d, 3] = g_ref[:, rest]
        out_ref[d, 4] = k_ref[:, head]
        out_ref[d, 5] = v_ref[:, head]


def pack(queries, out_grad, keys, values, lanes, count=8):
    tok = queries.shape[1]
    repeat = lanes // KV
    wide = pl.BlockSpec((None, tok, 2 * HD * count), lambda d: (0, 0, d))
    narrow = pl.BlockSpec((None, tok, HD * count // repeat), lambda d: (0, 0, d))
    return pl.pallas_call(
        functools.partial(pack_kernel, count, repeat),
        grid=(lanes // count,),
        in_specs=[wide, wide, narrow, narrow],
        out_specs=pl.BlockSpec((count, 6, tok, HD), lambda d: (d, 0, 0, 0)),
        out_shape=jax.ShapeDtypeStruct((lanes, 6, tok, HD), queries.dtype),
        compiler_params=pltpu.CompilerParams(dimension_semantics=("arbitrary",)),
        interpret=INTERPRET,
    )(queries, out_grad, keys, values)


def body(queries, keys, values, out_grad, window_blocks, global_blocks, random_blocks):
    lanes = lax.axis_size("seq")
    tok = queries.shape[1]
    repeat = lanes // KV
    send = pack(queries, out_grad, keys, values, lanes)
    packed = lax.all_to_all(send, "seq", split_axis=0, concat_axis=0, tiled=True)
    listed, live = block_lists(window_blocks, global_blocks, random_blocks)
    dq_first, acc = block_grads(packed, listed, live, 0)
    dq_first_next = from_behind(dq_first, "pipe", -1)
    dq_second, dkv = block_grads(packed, listed, live, 1, acc, jnp.bfloat16)
    dq_second_next = from_behind(dq_second, "pipe", -1)
    dkv_parts = lax.all_to_all(dkv, "seq", split_axis=0, concat_axis=0, tiled=True)
    dkv_wide = dkv_parts.reshape(KV, repeat, 2, tok, HD).astype(jnp.float32)
    dkv_sum = jnp.sum(dkv_wide, axis=1).astype(jnp.bfloat16)
    dk_tokens = dkv_sum[:, 0].transpose(1, 0, 2)
    dv_tokens = dkv_sum[:, 1].transpose(1, 0, 2)
    dk_flat = dk_tokens.reshape(1, tok, KV * HD)
    dv_flat = dv_tokens.reshape(1, tok, KV * HD)
    dk_next, dv_next = from_behind((dk_flat, dv_flat), "pipe", -1)
    dq_heads = jnp.concatenate([dq_first_next, dq_second_next], axis=2)
    dq_parts = lax.all_to_all(dq_heads, "seq", split_axis=0, concat_axis=0, tiled=True)
    dq_next = dq_parts.transpose(2, 0, 1, 3).reshape(1, tok, HEADS * HD)
    return dq_next, dk_next, dv_next


def solution(mesh):
    in_specs = (
        P("pipe", "seq", None),
        P("pipe", "seq", None),
        P("pipe", "seq", None),
        P("pipe", "seq", None),
        P(),
        P(),
        P(),
    )
    out_specs = (P("pipe", "seq", None), P("pipe", "seq", None), P("pipe", "seq", None))

    return jax.shard_map(body, mesh=mesh, in_specs=in_specs, out_specs=out_specs, check_vma=False)
```

```python
import functools

import jax
import jax.numpy as jnp
from jax import lax
from jax.experimental import pallas as pl
from jax.experimental.pallas import tpu as pltpu
from jax.sharding import PartitionSpec as P


KV = 8
HD = 128
BLOCK = 64
INTERPRET = False


def from_behind(block, axis, distance):
    devices = range(lax.axis_size(axis))
    route = [(i - distance, i) for i in devices if i - distance in devices]
    return lax.ppermute(block, axis, route)


def block_lists(window_blocks, global_blocks, random_blocks):
    listed = jnp.concatenate([window_blocks, global_blocks, random_blocks], axis=1)
    width = listed.shape[1]
    same = listed[:, :, None] == listed[:, None, :]
    earlier = jnp.arange(width)[None, :] < jnp.arange(width)[:, None]
    repeated = jnp.any(jnp.logical_and(same, earlier[None]), axis=2)
    return (listed, jnp.logical_not(repeated))


def grads_kernel(slots, steps, part, chained, listed_ref, live_ref, q_ref, g_ref, kv_ref, *refs):
    if chained:
        acc_in_ref, dq_ref, out_ref, kc_ref, vc_ref, dkv_ref = refs
    else:
        dq_ref, out_ref, kc_ref, vc_ref, dkv_ref = refs
    b = pl.program_id(0)
    scale = HD ** (-0.5)
    width = slots * BLOCK
    half = kv_ref.shape[2] // BLOCK

    @pl.when(b == 0)
    def _():
        if chained:
            dkv_ref[...] = acc_in_ref[...]
        else:
            dkv_ref[...] = jnp.zeros(dkv_ref.shape, dkv_ref.dtype)

    col = lax.broadcasted_iota(jnp.int32, (1, width), 1)
    nt = (((1,), (1,)), ((), ()))
    tn = (((0,), (0,)), ((), ()))
    for i in range(steps):
        base = ((b * steps + i) * half + part) * slots
        owners = []
        offsets = []
        lives = []
        for j in range(slots):
            n = listed_ref[base + j]
            owners.append(n // half)
            offsets.append(pl.multiple_of((n % half) * BLOCK, BLOCK))
            lives.append(live_ref[base + j])
            kc_ref[j * BLOCK:(j + 1) * BLOCK, :] = kv_ref[owners[j], 0, pl.ds(offsets[j], BLOCK), :]
            vc_ref[j * BLOCK:(j + 1) * BLOCK, :] = kv_ref[owners[j], 1, pl.ds(offsets[j], BLOCK), :]
        q = q_ref[i].reshape(-1, HD)
        g = g_ref[i].reshape(-1, HD)
        kc = kc_ref[...]
        vc = vc_ref[...]
        live_cols = jnp.zeros((1, width), jnp.int32)
        for j in range(slots):
            inside = jnp.logical_and(col >= j * BLOCK, col < (j + 1) * BLOCK)
            live_cols = jnp.where(inside, lives[j], live_cols)
        scores = lax.dot_general(q, kc, nt, preferred_element_type=jnp.float32) * scale
        scores = jnp.where(live_cols != 0, scores, -jnp.inf)
        top = jnp.max(scores, axis=-1, keepdims=True)
        expd = jnp.exp(scores - top)
        probs = expd / jnp.sum(expd, axis=-1, keepdims=True)
        probs_low = probs.astype(jnp.bfloat16)
        attn = jnp.dot(probs_low, vc, preferred_element_type=jnp.float32)
        attn = attn.astype(jnp.bfloat16).astype(jnp.float32)
        delta = jnp.sum(g.astype(jnp.float32) * attn, axis=-1, keepdims=True)
        dprobs = lax.dot_general(g, vc, nt, preferred_element_type=jnp.float32)
        ds_low = (probs * (dprobs - delta)).astype(jnp.bfloat16)
        dq = jnp.dot(ds_low, kc, preferred_element_type=jnp.float32) * scale
        dq_ref[i] = dq.astype(jnp.bfloat16).reshape(dq_ref.shape[1:])
        dk_slots = lax.dot_general(ds_low, q, tn, preferred_element_type=jnp.float32) * scale
        dv_slots = lax.dot_general(probs_low, g, tn, preferred_element_type=jnp.float32)
        for j in range(slots):
            @pl.when(lives[j] != 0)
            def _():
                window = pl.ds(offsets[j], BLOCK)
                dkv_ref[owners[j], 0, window, :] += dk_slots[j * BLOCK:(j + 1) * BLOCK, :]
                dkv_ref[owners[j], 1, window, :] += dv_slots[j * BLOCK:(j + 1) * BLOCK, :]

    @pl.when(b == pl.num_programs(0) - 1)
    def _():
        out_ref[...] = dkv_ref[...].astype(out_ref.dtype)


def block_grads(packed, listed, live, part, acc_in=None, out_dtype=jnp.float32, steps=4):
    nblocks, slots = listed.shape
    lanes, _, tok, _ = packed.shape
    per_device = 2
    width = slots * BLOCK
    chained = acc_in is not None
    kernel = functools.partial(grads_kernel, slots, steps, part, chained)
    whole = lambda b, *_: (0, 0, 0, 0)
    in_specs = [
        pl.BlockSpec((steps, per_device, BLOCK, HD), lambda b, *_: (b, 0, part, 0)),
        pl.BlockSpec((steps, per_device, BLOCK, HD), lambda b, *_: (b, 1, part, 0)),
        pl.BlockSpec((lanes, 2, tok, HD), lambda b, *_: (0, 2, 0, 0)),
    ]
    operands = [packed, packed, packed]
    if chained:
        in_specs.append(pl.BlockSpec((lanes, 2, tok, HD), whole))
        operands.append(acc_in)
    grid_spec = pltpu.PrefetchScalarGridSpec(
        num_scalar_prefetch=2,
        grid=(lanes // steps,),
        in_specs=in_specs,
        out_specs=[
            pl.BlockSpec((steps, per_device, BLOCK, HD), lambda b, *_: (b, 0, 0, 0)),
            pl.BlockSpec((lanes, 2, tok, HD), whole),
        ],
        scratch_shapes=[
            pltpu.VMEM((width, HD), jnp.bfloat16),
            pltpu.VMEM((width, HD), jnp.bfloat16),
            pltpu.VMEM((lanes, 2, tok, HD), jnp.float32),
        ],
    )
    return pl.pallas_call(
        kernel,
        grid_spec=grid_spec,
        out_shape=[
            jax.ShapeDtypeStruct((lanes, per_device, BLOCK, HD), jnp.bfloat16),
            jax.ShapeDtypeStruct((lanes, 2, tok, HD), out_dtype),
        ],
        compiler_params=pltpu.CompilerParams(dimension_semantics=("arbitrary",)),
        cost_estimate=pl.CostEstimate(
            flops=6 * nblocks * BLOCK * per_device * width * HD,
            transcendentals=nblocks * BLOCK * per_device * width // 2,
            bytes_accessed=3 * packed.size,
        ),
        interpret=INTERPRET,
    )(listed.reshape(-1), live.reshape(-1).astype(jnp.int32), *operands)


def pack_kernel(count, repeat, q_ref, g_ref, k_ref, v_ref, out_ref):
    for d in range(count):
        lead = slice(2 * d * HD, 2 * d * HD + HD)
        rest = slice(2 * d * HD + HD, 2 * (d + 1) * HD)
        head = slice(d // repeat * HD, (d // repeat + 1) * HD)
        out_ref[d, 0] = q_ref[:, lead]
        out_ref[d, 1] = q_ref[:, rest]
        out_ref[d, 2] = g_ref[:, lead]
        out_ref[d, 3] = g_ref[:, rest]
        out_ref[d, 4] = k_ref[:, head]
        out_ref[d, 5] = v_ref[:, head]


def pack(queries, out_grad, keys, values, lanes, count=8):
    tok = queries.shape[1]
    repeat = lanes // KV
    wide = pl.BlockSpec((None, tok, 2 * HD * count), lambda d: (0, 0, d))
    narrow = pl.BlockSpec((None, tok, HD * count // repeat), lambda d: (0, 0, d))
    return pl.pallas_call(
        functools.partial(pack_kernel, count, repeat),
        grid=(lanes // count,),
        in_specs=[wide, wide, narrow, narrow],
        out_specs=pl.BlockSpec((count, 6, tok, HD), lambda d: (d, 0, 0, 0)),
        out_shape=jax.ShapeDtypeStruct((lanes, 6, tok, HD), queries.dtype),
        compiler_params=pltpu.CompilerParams(dimension_semantics=("arbitrary",)),
        interpret=INTERPRET,
    )(queries, out_grad, keys, values)


def unpack_kernel(count, src_ref, out_ref):
    for p in range(count):
        out_ref[:, 2 * p * HD:2 * p * HD + HD] = src_ref[p, 0]
        out_ref[:, 2 * p * HD + HD:2 * (p + 1) * HD] = src_ref[p, 1]


def unpack(parts, count=8):
    lanes, per_device, tok, _ = parts.shape
    return pl.pallas_call(
        functools.partial(unpack_kernel, count),
        grid=(lanes // count,),
        in_specs=[pl.BlockSpec((count, per_device, tok, HD), lambda d: (d, 0, 0, 0))],
        out_specs=pl.BlockSpec((None, tok, per_device * HD * count), lambda d: (0, 0, d)),
        out_shape=jax.ShapeDtypeStruct((1, tok, lanes * per_device * HD), parts.dtype),
        compiler_params=pltpu.CompilerParams(dimension_semantics=("arbitrary",)),
        interpret=INTERPRET,
    )(parts)


def body(queries, keys, values, out_grad, window_blocks, global_blocks, random_blocks):
    lanes = lax.axis_size("seq")
    tok = queries.shape[1]
    repeat = lanes // KV
    send = pack(queries, out_grad, keys, values, lanes)
    packed = lax.all_to_all(send, "seq", split_axis=0, concat_axis=0, tiled=True)
    listed, live = block_lists(window_blocks, global_blocks, random_blocks)
    dq_first, acc = block_grads(packed, listed, live, 0)
    dq_first_next = from_behind(dq_first, "pipe", -1)
    dq_second, dkv = block_grads(packed, listed, live, 1, acc, jnp.bfloat16)
    dq_second_next = from_behind(dq_second, "pipe", -1)
    dkv_parts = lax.all_to_all(dkv, "seq", split_axis=0, concat_axis=0, tiled=True)
    dkv_wide = dkv_parts.reshape(KV, repeat, 2, tok, HD).astype(jnp.float32)
    dkv_sum = jnp.sum(dkv_wide, axis=1).astype(jnp.bfloat16)
    dk_tokens = dkv_sum[:, 0].transpose(1, 0, 2)
    dv_tokens = dkv_sum[:, 1].transpose(1, 0, 2)
    dk_flat = dk_tokens.reshape(1, tok, KV * HD)
    dv_flat = dv_tokens.reshape(1, tok, KV * HD)
    dk_next, dv_next = from_behind((dk_flat, dv_flat), "pipe", -1)
    dq_heads = jnp.concatenate([dq_first_next, dq_second_next], axis=2)
    dq_parts = lax.all_to_all(dq_heads, "seq", split_axis=0, concat_axis=0, tiled=True)
    dq_next = unpack(dq_parts)
    return dq_next, dk_next, dv_next


def solution(mesh):
    in_specs = (
        P("pipe", "seq", None),
        P("pipe", "seq", None),
        P("pipe", "seq", None),
        P("pipe", "seq", None),
        P(),
        P(),
        P(),
    )
    out_specs = (P("pipe", "seq", None), P("pipe", "seq", None), P("pipe", "seq", None))

    return jax.shard_map(body, mesh=mesh, in_specs=in_specs, out_specs=out_specs, check_vma=False)
```

```python
import functools

import jax
import jax.numpy as jnp
from jax import lax
from jax.experimental import pallas as pl
from jax.experimental.pallas import tpu as pltpu
from jax.sharding import PartitionSpec as P


KV = 8
HD = 128
BLOCK = 64
INTERPRET = False


def from_behind(block, axis, distance):
    devices = range(lax.axis_size(axis))
    route = [(i - distance, i) for i in devices if i - distance in devices]
    return lax.ppermute(block, axis, route)


def block_lists(window_blocks, global_blocks, random_blocks):
    listed = jnp.concatenate([window_blocks, global_blocks, random_blocks], axis=1)
    width = listed.shape[1]
    same = listed[:, :, None] == listed[:, None, :]
    earlier = jnp.arange(width)[None, :] < jnp.arange(width)[:, None]
    repeated = jnp.any(jnp.logical_and(same, earlier[None]), axis=2)
    return (listed, jnp.logical_not(repeated))


def grads_kernel(slots, steps, part, chained, listed_ref, live_ref, q_ref, g_ref, kv_ref, *refs):
    if chained:
        acc_in_ref, dq_ref, out_ref, kc_ref, vc_ref, dkv_ref = refs
    else:
        dq_ref, out_ref, kc_ref, vc_ref, dkv_ref = refs
    b = pl.program_id(0)
    scale = HD ** (-0.5)
    width = slots * BLOCK
    half = kv_ref.shape[2] // BLOCK

    @pl.when(b == 0)
    def _():
        if chained:
            dkv_ref[...] = acc_in_ref[...]
        else:
            dkv_ref[...] = jnp.zeros(dkv_ref.shape, dkv_ref.dtype)

    col = lax.broadcasted_iota(jnp.int32, (1, width), 1)
    nt = (((1,), (1,)), ((), ()))
    tn = (((0,), (0,)), ((), ()))
    for i in range(steps):
        base = ((b * steps + i) * half + part) * slots
        owners = []
        offsets = []
        lives = []
        for j in range(slots):
            n = listed_ref[base + j]
            owners.append(n // half)
            offsets.append(pl.multiple_of((n % half) * BLOCK, BLOCK))
            lives.append(live_ref[base + j])
            kc_ref[j * BLOCK:(j + 1) * BLOCK, :] = kv_ref[owners[j], 0, pl.ds(offsets[j], BLOCK), :]
            vc_ref[j * BLOCK:(j + 1) * BLOCK, :] = kv_ref[owners[j], 1, pl.ds(offsets[j], BLOCK), :]
        q = q_ref[i].reshape(-1, HD)
        g = g_ref[i].reshape(-1, HD)
        kc = kc_ref[...]
        vc = vc_ref[...]
        live_cols = jnp.zeros((1, width), jnp.int32)
        for j in range(slots):
            inside = jnp.logical_and(col >= j * BLOCK, col < (j + 1) * BLOCK)
            live_cols = jnp.where(inside, lives[j], live_cols)
        scores = lax.dot_general(q, kc, nt, preferred_element_type=jnp.float32) * scale
        scores = jnp.where(live_cols != 0, scores, -jnp.inf)
        top = jnp.max(scores, axis=-1, keepdims=True)
        expd = jnp.exp(scores - top)
        probs = expd / jnp.sum(expd, axis=-1, keepdims=True)
        probs_low = probs.astype(jnp.bfloat16)
        attn = jnp.dot(probs_low, vc, preferred_element_type=jnp.float32)
        attn = attn.astype(jnp.bfloat16).astype(jnp.float32)
        delta = jnp.sum(g.astype(jnp.float32) * attn, axis=-1, keepdims=True)
        dprobs = lax.dot_general(g, vc, nt, preferred_element_type=jnp.float32)
        ds_low = (probs * (dprobs - delta)).astype(jnp.bfloat16)
        dq = jnp.dot(ds_low, kc, preferred_element_type=jnp.float32) * scale
        dq_ref[i] = dq.astype(jnp.bfloat16).reshape(dq_ref.shape[1:])
        dk_slots = lax.dot_general(ds_low, q, tn, preferred_element_type=jnp.float32) * scale
        dv_slots = lax.dot_general(probs_low, g, tn, preferred_element_type=jnp.float32)
        for j in range(slots):
            @pl.when(lives[j] != 0)
            def _():
                window = pl.ds(offsets[j], BLOCK)
                dkv_ref[owners[j], 0, window, :] += dk_slots[j * BLOCK:(j + 1) * BLOCK, :]
                dkv_ref[owners[j], 1, window, :] += dv_slots[j * BLOCK:(j + 1) * BLOCK, :]

    @pl.when(b == pl.num_programs(0) - 1)
    def _():
        out_ref[...] = dkv_ref[...].astype(out_ref.dtype)


def block_grads(packed, listed, live, part, acc_in=None, out_dtype=jnp.float32, steps=4):
    nblocks, slots = listed.shape
    lanes, _, tok, _ = packed.shape
    per_device = 2
    width = slots * BLOCK
    chained = acc_in is not None
    kernel = functools.partial(grads_kernel, slots, steps, part, chained)
    whole = lambda b, *_: (0, 0, 0, 0)
    in_specs = [
        pl.BlockSpec((steps, per_device, BLOCK, HD), lambda b, *_: (b, 0, part, 0)),
        pl.BlockSpec((steps, per_device, BLOCK, HD), lambda b, *_: (b, 1, part, 0)),
        pl.BlockSpec((lanes, 2, tok, HD), lambda b, *_: (0, 2, 0, 0)),
    ]
    operands = [packed, packed, packed]
    if chained:
        in_specs.append(pl.BlockSpec((lanes, 2, tok, HD), whole))
        operands.append(acc_in)
    grid_spec = pltpu.PrefetchScalarGridSpec(
        num_scalar_prefetch=2,
        grid=(lanes // steps,),
        in_specs=in_specs,
        out_specs=[
            pl.BlockSpec((steps, per_device, BLOCK, HD), lambda b, *_: (b, 0, 0, 0)),
            pl.BlockSpec((lanes, 2, tok, HD), whole),
        ],
        scratch_shapes=[
            pltpu.VMEM((width, HD), jnp.bfloat16),
            pltpu.VMEM((width, HD), jnp.bfloat16),
            pltpu.VMEM((lanes, 2, tok, HD), jnp.float32),
        ],
    )
    return pl.pallas_call(
        kernel,
        grid_spec=grid_spec,
        out_shape=[
            jax.ShapeDtypeStruct((lanes, per_device, BLOCK, HD), jnp.bfloat16),
            jax.ShapeDtypeStruct((lanes, 2, tok, HD), out_dtype),
        ],
        compiler_params=pltpu.CompilerParams(dimension_semantics=("arbitrary",)),
        cost_estimate=pl.CostEstimate(
            flops=6 * nblocks * BLOCK * per_device * width * HD,
            transcendentals=nblocks * BLOCK * per_device * width // 2,
            bytes_accessed=3 * packed.size,
        ),
        interpret=INTERPRET,
    )(listed.reshape(-1), live.reshape(-1).astype(jnp.int32), *operands)


def pack_kernel(count, repeat, q_ref, g_ref, k_ref, v_ref, out_ref):
    for d in range(count):
        lead = slice(2 * d * HD, 2 * d * HD + HD)
        rest = slice(2 * d * HD + HD, 2 * (d + 1) * HD)
        head = slice(d // repeat * HD, (d // repeat + 1) * HD)
        out_ref[d, 0] = q_ref[:, lead]
        out_ref[d, 1] = q_ref[:, rest]
        out_ref[d, 2] = g_ref[:, lead]
        out_ref[d, 3] = g_ref[:, rest]
        out_ref[d, 4] = k_ref[:, head]
        out_ref[d, 5] = v_ref[:, head]


def pack(queries, out_grad, keys, values, lanes, count=8):
    tok = queries.shape[1]
    repeat = lanes // KV
    wide = pl.BlockSpec((None, tok, 2 * HD * count), lambda d: (0, 0, d))
    narrow = pl.BlockSpec((None, tok, HD * count // repeat), lambda d: (0, 0, d))
    return pl.pallas_call(
        functools.partial(pack_kernel, count, repeat),
        grid=(lanes // count,),
        in_specs=[wide, wide, narrow, narrow],
        out_specs=pl.BlockSpec((count, 6, tok, HD), lambda d: (d, 0, 0, 0)),
        out_shape=jax.ShapeDtypeStruct((lanes, 6, tok, HD), queries.dtype),
        compiler_params=pltpu.CompilerParams(dimension_semantics=("arbitrary",)),
        interpret=INTERPRET,
    )(queries, out_grad, keys, values)


def unpack_kernel(count, src_ref, out_ref):
    for p in range(count):
        out_ref[:, 2 * p * HD:2 * p * HD + HD] = src_ref[p, 0]
        out_ref[:, 2 * p * HD + HD:2 * (p + 1) * HD] = src_ref[p, 1]


def unpack(parts, count=8):
    lanes, per_device, tok, _ = parts.shape
    return pl.pallas_call(
        functools.partial(unpack_kernel, count),
        grid=(lanes // count,),
        in_specs=[pl.BlockSpec((count, per_device, tok, HD), lambda d: (d, 0, 0, 0))],
        out_specs=pl.BlockSpec((None, tok, per_device * HD * count), lambda d: (0, 0, d)),
        out_shape=jax.ShapeDtypeStruct((1, tok, lanes * per_device * HD), parts.dtype),
        compiler_params=pltpu.CompilerParams(dimension_semantics=("arbitrary",)),
        interpret=INTERPRET,
    )(parts)


def body(queries, keys, values, out_grad, window_blocks, global_blocks, random_blocks):
    lanes = lax.axis_size("seq")
    tok = queries.shape[1]
    repeat = lanes // KV
    send = pack(queries, out_grad, keys, values, lanes)
    packed = lax.all_to_all(send, "seq", split_axis=0, concat_axis=0, tiled=True)
    listed, live = block_lists(window_blocks, global_blocks, random_blocks)
    dq_first, acc = block_grads(packed, listed, live, 0)
    dq_first_next = from_behind(dq_first, "pipe", -1)
    dq_second, dkv = block_grads(packed, listed, live, 1, acc, jnp.bfloat16)
    dq_second_tok = lax.all_to_all(dq_second, "seq", split_axis=0, concat_axis=0, tiled=True)
    dq_second_next = from_behind(dq_second_tok, "pipe", -1)
    dkv_parts = lax.all_to_all(dkv, "seq", split_axis=0, concat_axis=0, tiled=True)
    dkv_wide = dkv_parts.reshape(KV, repeat, 2, tok, HD).astype(jnp.float32)
    dkv_sum = jnp.sum(dkv_wide, axis=1).astype(jnp.bfloat16)
    dkv_tokens = dkv_sum.transpose(1, 2, 0, 3).reshape(2, tok, KV * HD)
    dkv_next = from_behind(dkv_tokens, "pipe", -1)
    dk_next = dkv_next[0:1]
    dv_next = dkv_next[1:2]
    dq_first_tok = lax.all_to_all(dq_first_next, "seq", split_axis=0, concat_axis=0, tiled=True)
    dq_parts = jnp.concatenate([dq_first_tok, dq_second_next], axis=2)
    dq_next = unpack(dq_parts)
    return dq_next, dk_next, dv_next


def solution(mesh):
    in_specs = (
        P("pipe", "seq", None),
        P("pipe", "seq", None),
        P("pipe", "seq", None),
        P("pipe", "seq", None),
        P(),
        P(),
        P(),
    )
    out_specs = (P("pipe", "seq", None), P("pipe", "seq", None), P("pipe", "seq", None))

    return jax.shard_map(body, mesh=mesh, in_specs=in_specs, out_specs=out_specs, check_vma=False)
```

```python
import functools

import jax
import jax.numpy as jnp
from jax import lax
from jax.experimental import pallas as pl
from jax.experimental.pallas import tpu as pltpu
from jax.sharding import PartitionSpec as P


KV = 8
HD = 128
BLOCK = 64
INTERPRET = False


def from_behind(block, axis, distance):
    devices = range(lax.axis_size(axis))
    route = [(i - distance, i) for i in devices if i - distance in devices]
    return lax.ppermute(block, axis, route)


def block_lists(window_blocks, global_blocks, random_blocks):
    listed = jnp.concatenate([window_blocks, global_blocks, random_blocks], axis=1)
    width = listed.shape[1]
    same = listed[:, :, None] == listed[:, None, :]
    earlier = jnp.arange(width)[None, :] < jnp.arange(width)[:, None]
    repeated = jnp.any(jnp.logical_and(same, earlier[None]), axis=2)
    return (listed, jnp.logical_not(repeated))


def grads_kernel(slots, steps, part, chained, listed_ref, live_ref, q_ref, g_ref, kv_ref, *refs):
    if chained:
        acc_in_ref, dq_ref, out_ref, kc_ref, vc_ref, dkv_ref = refs
    else:
        dq_ref, out_ref, kc_ref, vc_ref, dkv_ref = refs
    b = pl.program_id(0)
    scale = HD ** (-0.5)
    width = slots * BLOCK
    half = kv_ref.shape[2] // BLOCK

    @pl.when(b == 0)
    def _():
        if chained:
            dkv_ref[...] = acc_in_ref[...]
        else:
            dkv_ref[...] = jnp.zeros(dkv_ref.shape, dkv_ref.dtype)

    col = lax.broadcasted_iota(jnp.int32, (1, width), 1)
    nt = (((1,), (1,)), ((), ()))
    tn = (((0,), (0,)), ((), ()))
    for i in range(steps):
        base = ((b * steps + i) * half + part) * slots
        owners = []
        offsets = []
        lives = []
        for j in range(slots):
            n = listed_ref[base + j]
            owners.append(n // half)
            offsets.append(pl.multiple_of((n % half) * BLOCK, BLOCK))
            lives.append(live_ref[base + j])
            kc_ref[j * BLOCK:(j + 1) * BLOCK, :] = kv_ref[owners[j], 0, pl.ds(offsets[j], BLOCK), :]
            vc_ref[j * BLOCK:(j + 1) * BLOCK, :] = kv_ref[owners[j], 1, pl.ds(offsets[j], BLOCK), :]
        q = q_ref[i].reshape(-1, HD)
        g = g_ref[i].reshape(-1, HD)
        kc = kc_ref[...]
        vc = vc_ref[...]
        live_cols = jnp.zeros((1, width), jnp.int32)
        for j in range(slots):
            inside = jnp.logical_and(col >= j * BLOCK, col < (j + 1) * BLOCK)
            live_cols = jnp.where(inside, lives[j], live_cols)
        scores = lax.dot_general(q, kc, nt, preferred_element_type=jnp.float32) * scale
        scores = jnp.where(live_cols != 0, scores, -jnp.inf)
        top = jnp.max(scores, axis=-1, keepdims=True)
        expd = jnp.exp(scores - top)
        probs = expd / jnp.sum(expd, axis=-1, keepdims=True)
        probs_low = probs.astype(jnp.bfloat16)
        attn = jnp.dot(probs_low, vc, preferred_element_type=jnp.float32)
        attn = attn.astype(jnp.bfloat16).astype(jnp.float32)
        delta = jnp.sum(g.astype(jnp.float32) * attn, axis=-1, keepdims=True)
        dprobs = lax.dot_general(g, vc, nt, preferred_element_type=jnp.float32)
        ds_low = (probs * (dprobs - delta)).astype(jnp.bfloat16)
        dq = jnp.dot(ds_low, kc, preferred_element_type=jnp.float32) * scale
        dq_ref[i] = dq.astype(jnp.bfloat16).reshape(dq_ref.shape[1:])
        dk_slots = lax.dot_general(ds_low, q, tn, preferred_element_type=jnp.float32) * scale
        dv_slots = lax.dot_general(probs_low, g, tn, preferred_element_type=jnp.float32)
        for j in range(slots):
            @pl.when(lives[j] != 0)
            def _():
                window = pl.ds(offsets[j], BLOCK)
                dkv_ref[owners[j], 0, window, :] += dk_slots[j * BLOCK:(j + 1) * BLOCK, :]
                dkv_ref[owners[j], 1, window, :] += dv_slots[j * BLOCK:(j + 1) * BLOCK, :]

    @pl.when(b == pl.num_programs(0) - 1)
    def _():
        out_ref[...] = dkv_ref[...].astype(out_ref.dtype)


def block_grads(packed, listed, live, part, acc_in=None, out_dtype=jnp.float32, steps=8):
    nblocks, slots = listed.shape
    lanes, _, tok, _ = packed.shape
    per_device = 2
    width = slots * BLOCK
    chained = acc_in is not None
    kernel = functools.partial(grads_kernel, slots, steps, part, chained)
    whole = lambda b, *_: (0, 0, 0, 0)
    in_specs = [
        pl.BlockSpec((steps, per_device, BLOCK, HD), lambda b, *_: (b, 0, part, 0)),
        pl.BlockSpec((steps, per_device, BLOCK, HD), lambda b, *_: (b, 1, part, 0)),
        pl.BlockSpec((lanes, 2, tok, HD), lambda b, *_: (0, 2, 0, 0)),
    ]
    operands = [packed, packed, packed]
    if chained:
        in_specs.append(pl.BlockSpec((lanes, 2, tok, HD), whole))
        operands.append(acc_in)
    grid_spec = pltpu.PrefetchScalarGridSpec(
        num_scalar_prefetch=2,
        grid=(lanes // steps,),
        in_specs=in_specs,
        out_specs=[
            pl.BlockSpec((steps, per_device, BLOCK, HD), lambda b, *_: (b, 0, 0, 0)),
            pl.BlockSpec((lanes, 2, tok, HD), whole),
        ],
        scratch_shapes=[
            pltpu.VMEM((width, HD), jnp.bfloat16),
            pltpu.VMEM((width, HD), jnp.bfloat16),
            pltpu.VMEM((lanes, 2, tok, HD), jnp.float32),
        ],
    )
    return pl.pallas_call(
        kernel,
        grid_spec=grid_spec,
        out_shape=[
            jax.ShapeDtypeStruct((lanes, per_device, BLOCK, HD), jnp.bfloat16),
            jax.ShapeDtypeStruct((lanes, 2, tok, HD), out_dtype),
        ],
        compiler_params=pltpu.CompilerParams(dimension_semantics=("arbitrary",)),
        cost_estimate=pl.CostEstimate(
            flops=6 * nblocks * BLOCK * per_device * width * HD,
            transcendentals=nblocks * BLOCK * per_device * width // 2,
            bytes_accessed=3 * packed.size,
        ),
        interpret=INTERPRET,
    )(listed.reshape(-1), live.reshape(-1).astype(jnp.int32), *operands)


def pack_kernel(count, repeat, q_ref, g_ref, k_ref, v_ref, out_ref):
    for d in range(count):
        lead = slice(2 * d * HD, 2 * d * HD + HD)
        rest = slice(2 * d * HD + HD, 2 * (d + 1) * HD)
        head = slice(d // repeat * HD, (d // repeat + 1) * HD)
        out_ref[d, 0] = q_ref[:, lead]
        out_ref[d, 1] = q_ref[:, rest]
        out_ref[d, 2] = g_ref[:, lead]
        out_ref[d, 3] = g_ref[:, rest]
        out_ref[d, 4] = k_ref[:, head]
        out_ref[d, 5] = v_ref[:, head]


def pack(queries, out_grad, keys, values, lanes, count=8):
    tok = queries.shape[1]
    repeat = lanes // KV
    wide = pl.BlockSpec((None, tok, 2 * HD * count), lambda d: (0, 0, d))
    narrow = pl.BlockSpec((None, tok, HD * count // repeat), lambda d: (0, 0, d))
    return pl.pallas_call(
        functools.partial(pack_kernel, count, repeat),
        grid=(lanes // count,),
        in_specs=[wide, wide, narrow, narrow],
        out_specs=pl.BlockSpec((count, 6, tok, HD), lambda d: (d, 0, 0, 0)),
        out_shape=jax.ShapeDtypeStruct((lanes, 6, tok, HD), queries.dtype),
        compiler_params=pltpu.CompilerParams(dimension_semantics=("arbitrary",)),
        interpret=INTERPRET,
    )(queries, out_grad, keys, values)


def unpack_kernel(count, src_ref, out_ref):
    for p in range(count):
        out_ref[:, 2 * p * HD:2 * p * HD + HD] = src_ref[p, 0]
        out_ref[:, 2 * p * HD + HD:2 * (p + 1) * HD] = src_ref[p, 1]


def unpack(parts, count=8):
    lanes, per_device, tok, _ = parts.shape
    return pl.pallas_call(
        functools.partial(unpack_kernel, count),
        grid=(lanes // count,),
        in_specs=[pl.BlockSpec((count, per_device, tok, HD), lambda d: (d, 0, 0, 0))],
        out_specs=pl.BlockSpec((None, tok, per_device * HD * count), lambda d: (0, 0, d)),
        out_shape=jax.ShapeDtypeStruct((1, tok, lanes * per_device * HD), parts.dtype),
        compiler_params=pltpu.CompilerParams(dimension_semantics=("arbitrary",)),
        interpret=INTERPRET,
    )(parts)


def body(queries, keys, values, out_grad, window_blocks, global_blocks, random_blocks):
    lanes = lax.axis_size("seq")
    tok = queries.shape[1]
    repeat = lanes // KV
    send = pack(queries, out_grad, keys, values, lanes)
    packed = lax.all_to_all(send, "seq", split_axis=0, concat_axis=0, tiled=True)
    listed, live = block_lists(window_blocks, global_blocks, random_blocks)
    dq_first, acc = block_grads(packed, listed, live, 0)
    dq_first_next = from_behind(dq_first, "pipe", -1)
    dq_second, dkv = block_grads(packed, listed, live, 1, acc, jnp.bfloat16)
    dq_second_next = from_behind(dq_second, "pipe", -1)
    dkv_parts = lax.all_to_all(dkv, "seq", split_axis=0, concat_axis=0, tiled=True)
    dkv_wide = dkv_parts.reshape(KV, repeat, 2, tok, HD).astype(jnp.float32)
    dkv_sum = jnp.sum(dkv_wide, axis=1).astype(jnp.bfloat16)
    dkv_tokens = dkv_sum.transpose(1, 2, 0, 3).reshape(2, tok, KV * HD)
    dkv_next = from_behind(dkv_tokens, "pipe", -1)
    dk_next = dkv_next[0:1]
    dv_next = dkv_next[1:2]
    dq_heads = jnp.concatenate([dq_first_next, dq_second_next], axis=2)
    dq_parts = lax.all_to_all(dq_heads, "seq", split_axis=0, concat_axis=0, tiled=True)
    dq_next = unpack(dq_parts)
    return dq_next, dk_next, dv_next


def solution(mesh):
    in_specs = (
        P("pipe", "seq", None),
        P("pipe", "seq", None),
        P("pipe", "seq", None),
        P("pipe", "seq", None),
        P(),
        P(),
        P(),
    )
    out_specs = (P("pipe", "seq", None), P("pipe", "seq", None), P("pipe", "seq", None))

    return jax.shard_map(body, mesh=mesh, in_specs=in_specs, out_specs=out_specs, check_vma=False)
```
